32 devices in a mesh: node: 4 (over z), local: 8 (over y, x, core).
Axes of the slice: x: 2, y: 2, z: 4, core: 2. Of those that a mesh axis runs over, the one named last changes fastest.
Arguments:
- hidden_in: bfloat16 [4096, 3584], P(('node', 'local')), may hold values from -6 to 6
- out_grad: bfloat16 [4096, 3584], P(('node', 'local')), may hold values from -6 to 6
- expert_ids: int32 [4, 1024, 8], P(None, 'local'), may hold values from 0 to 31, as said below
- gate_int: int32 [4, 1024, 8], P(None, 'local'), may hold values from 1 to 256
- gate_saved: bfloat16 [32768, 1024], P(('node', 'local')), may hold values from -6 to 6
- w_in: bfloat16 [32, 3584, 2048], P(('node', 'local')), may hold values from -0.09375 to 0.09375
- w_out: bfloat16 [32, 1024, 3584], P(('node', 'local')), may hold values from -0.1875 to 0.1875
Outputs:
- grad_in: bfloat16 [4096, 3584], P(('node', 'local'))
The draws below stay inside these ranges and needn't reach their ends.
Inputs may be any that keep to these rules, and one draw needn't show every extreme that they name: `expert_ids`: each token names 8 different experts, two on each of 4 different nodes. Among the 128 tokens of one device (one n, one value of j // 128) every expert is named exactly 32 times.
All inputs are finite; a program needn't handle non-finite values.
Results may differ from the reference program's by a relative error of at most 0.0085.
Values may be sent and summed in bfloat16 or wider, within the bound.
No kernel may reach another device: no remote copies, remote signals or barrier semaphores. Data moves between devices by JAX's collectives and lax.ppermute only.
A program may use at most 128 MiB of HBM per device.

```python
import jax
import jax.numpy as jnp
from jax import lax

D = 3584
FF = 1024
TOK_DEV = 128
TOPK = 8
NODE_LIMIT = 4
EXPERTS = 32
TOKENS = 4096
ROWS_EXP = 1024
N_NODE = 4
N_LOCAL = 8


def draw_expert_ids(key, part):
    devices_all = N_NODE * N_LOCAL
    subkeys = jax.random.split(jax.random.fold_in(key, 7), 5)
    scores = jax.random.randint(subkeys[0], (devices_all, TOK_DEV), 0, 1 << 20)
    ranked = scores * TOK_DEV + jnp.arange(TOK_DEV, dtype=jnp.int32)[None, :]
    shuffle = jnp.argsort(ranked, axis=1).astype(jnp.int32)
    digit_low = shuffle % N_NODE
    column = shuffle // N_NODE
    stride_bit = column % (N_NODE // 2)
    shift = jax.random.randint(subkeys[1], (devices_all, 1, 1), 0, N_NODE)
    offsets = jax.random.randint(subkeys[2], (devices_all, 1, NODE_LIMIT), 0, N_LOCAL)
    strides = jax.random.randint(subkeys[3], (devices_all, 1, NODE_LIMIT), 1, N_LOCAL)
    slot_range = jnp.arange(NODE_LIMIT, dtype=jnp.int32)[None, None, :]
    nodes = (digit_low[:, :, None] + slot_range * (2 * stride_bit[:, :, None] + 1) + shift) % N_NODE
    first_local = (column[:, :, None] + offsets) % N_LOCAL
    second_local = (first_local + strides) % N_LOCAL
    paired = jnp.stack([nodes * N_LOCAL + first_local, nodes * N_LOCAL + second_local], axis=-1)
    experts = paired.reshape(devices_all, TOK_DEV, TOPK)
    slot_scores = jax.random.randint(subkeys[4], (devices_all, TOK_DEV, TOPK), 0, 1 << 20)
    slot_scores = slot_scores * TOPK + jnp.arange(TOPK, dtype=jnp.int32)
    slot_perm = jnp.argsort(slot_scores, axis=-1)
    experts = jnp.take_along_axis(experts, slot_perm, axis=-1)
    return experts.reshape(N_NODE, N_LOCAL * TOK_DEV, TOPK).astype(jnp.int32)


def plant(values, own_key, low, top_value):
    shape = values.shape
    place = [jax.random.randint(jax.random.fold_in(own_key, axis), (), 0, shape[axis]) for axis in range(len(shape))]
    values = values.at[tuple(place)].set(low)
    longest = shape.index(max(shape))
    place[longest] = (place[longest] + 1) % shape[longest]
    return values.at[tuple(place)].set(top_value)


def block_levels(stream_key, dims, cuts, least, high):
    def one(dim, parts):
        steps = jax.random.uniform(jax.random.fold_in(jax.random.fold_in(stream_key, 6), dim), (parts,), jnp.float32, least / len(cuts), high / len(cuts))
        return jnp.repeat(jnp.exp(steps), dims[dim] // parts).reshape((-1,) + (1,) * (len(dims) - dim - 1))

    gain = one(*cuts[0])
    for cut in cuts[1:]:
        gain = gain * one(*cut)
    return gain


def gaussian(own_key, dims, width, most, cuts=(), held_as=jnp.bfloat16):
    result = jax.random.normal(own_key, dims, jnp.float32) * width
    if len(cuts) > 0:
        result = block_levels(own_key, dims, cuts, -0.22, 0.18) * result
    return jnp.clip(result, min=-most, max=most).astype(held_as)


def setup_inputs(seed: int = 0) -> dict:
    arg_keys = jax.random.split(jax.random.key(seed), 8)
    hidden_in = gaussian(arg_keys[0], (TOKENS, D), 1.0, 6.0, ((0, 32),))
    out_grad = gaussian(arg_keys[1], (TOKENS, D), 1.0, 6.0, ((0, 32),))
    expert_ids = draw_expert_ids(jax.random.fold_in(arg_keys[7], 71), 0)
    gate_int = plant(jax.random.randint(arg_keys[3], (N_NODE, N_LOCAL * TOK_DEV, TOPK), 1, 257), jax.random.fold_in(arg_keys[3], 1), 1, 256).astype(jnp.int32)
    gate_saved = gaussian(arg_keys[4], (EXPERTS * ROWS_EXP, FF), 1.5, 6.0, ((0, 32),))
    w_in = gaussian(arg_keys[5], (EXPERTS, D, 2 * FF), D ** -0.5, 0.09375, ((0, 32),))
    w_out = gaussian(arg_keys[6], (EXPERTS, FF, D), FF ** -0.5, 0.1875, ((0, 32),))
    return {"hidden_in": hidden_in, "out_grad": out_grad, "expert_ids": expert_ids, "gate_int": gate_int, "gate_saved": gate_saved, "w_in": w_in, "w_out": w_out}


def expert_part(rows_x, rows_dy, row_weight, saved, weight_in, weight_out):
    up_pre = jnp.dot(rows_x, weight_in[:, FF:], preferred_element_type=jnp.float32)
    grad_hidden = jnp.dot(rows_dy, weight_out.T, preferred_element_type=jnp.float32)
    grad_hidden = grad_hidden * row_weight[:, None]
    gate_pre = saved.astype(jnp.float32)
    sigmoid_gate = jax.nn.sigmoid(gate_pre)
    grad_gate = grad_hidden * up_pre * sigmoid_gate * (1.0 + gate_pre * (1.0 - sigmoid_gate))
    grad_up = grad_hidden * gate_pre * sigmoid_gate
    grad_pre = jnp.concatenate([grad_gate, grad_up], axis=1).astype(jnp.bfloat16)
    return jnp.dot(grad_pre, weight_in.T, preferred_element_type=jnp.float32).astype(jnp.bfloat16)


def reference(hidden_in, out_grad, expert_ids, gate_int, gate_saved, w_in, w_out):
    rows_exp = TOPK * TOK_DEV
    flat_ids = expert_ids.reshape(-1).astype(jnp.int32)
    weight = gate_int.reshape(-1).astype(jnp.float32) / 1024.0
    slot_order = jnp.argsort(flat_ids, stable=True).astype(jnp.int32)
    model_width = hidden_in.shape[1]

    def node_pass(summed, node_index):
        def expert_pass(partial_value, local_index):
            expert = node_index * N_LOCAL + local_index
            chosen = lax.dynamic_slice(slot_order, (expert * rows_exp,), (rows_exp,))
            tokens = chosen // TOPK
            saved = lax.dynamic_slice_in_dim(gate_saved, expert * rows_exp, rows_exp, 0)
            contrib = expert_part(hidden_in[tokens], out_grad[tokens], weight[chosen], saved, w_in[expert], w_out[expert])
            return partial_value.at[tokens].add(contrib.astype(jnp.float32)), None

        partial_value, _ = lax.scan(expert_pass, jnp.zeros((TOKENS, model_width), jnp.float32), jnp.arange(N_LOCAL, dtype=jnp.int32))
        rounded = lax.optimization_barrier(partial_value.astype(jnp.bfloat16))
        return summed + rounded.astype(jnp.float32), None

    summed, _ = lax.scan(node_pass, jnp.zeros((TOKENS, model_width), jnp.float32), jnp.arange(N_NODE, dtype=jnp.int32))
    return summed.astype(jnp.bfloat16)
```

```python
import jax
import jax.numpy as jnp
from jax import lax
from jax.sharding import PartitionSpec as P

FF = 1024
TOK_DEV = 128
TOPK = 8


def slot_ranks(flat_ids, columns):
    onehot = (flat_ids[..., None] == jnp.arange(columns, dtype=jnp.int32)).astype(jnp.int32)
    counts = jnp.cumsum(onehot, axis=-2)
    return jnp.sum(counts * onehot, axis=-1) - 1


def expert_backward(rows_x, rows_dy, rows_gate, saved, weight_in, weight_out):
    up_pre = jnp.dot(rows_x, weight_in[:, FF:], preferred_element_type=jnp.float32)
    grad_hidden = lax.dot_general(
        rows_dy, weight_out, (((1,), (1,)), ((), ())), preferred_element_type=jnp.float32
    )
    grad_hidden = grad_hidden * rows_gate.astype(jnp.float32)[:, None]
    gate_pre = saved.astype(jnp.float32)
    sigmoid_gate = jax.nn.sigmoid(gate_pre)
    grad_gate = grad_hidden * up_pre * sigmoid_gate * (1.0 + gate_pre * (1.0 - sigmoid_gate))
    grad_up = grad_hidden * gate_pre * sigmoid_gate
    grad_pre = jnp.concatenate([grad_gate, grad_up], axis=1).astype(jnp.bfloat16)
    contrib = lax.dot_general(
        grad_pre, weight_in, (((1,), (1,)), ((), ())), preferred_element_type=jnp.float32
    )
    return contrib.astype(jnp.bfloat16)


def on_device(hidden_in, out_grad, expert_ids, gate_int, gate_saved, w_in, w_out):
    n_node = lax.axis_size("node")
    n_local = lax.axis_size("local")
    experts = n_node * n_local
    tok = hidden_in.shape[0]
    capacity = tok * TOPK // experts
    per_dest = n_node * capacity
    row_count = n_local * per_dest
    model_width = hidden_in.shape[1]
    node_here = lax.axis_index("node")

    gathered_x = lax.all_gather(hidden_in, "node", tiled=True)
    gathered_dy = lax.all_gather(out_grad, "node", tiled=True)

    ids = expert_ids.reshape(n_node, tok * TOPK)
    ranks = slot_ranks(ids, experts)
    on_here = (ids // n_local) == node_here
    node_range = jnp.arange(n_node, dtype=jnp.int32)[:, None]
    position = (ids % n_local) * per_dest + node_range * capacity + ranks
    position = jnp.where(on_here, position, row_count)
    flat_slot = jnp.arange(n_node * tok * TOPK, dtype=jnp.int32)
    slot_of_row = (
        jnp.zeros((row_count,), jnp.int32).at[position.reshape(-1)].set(flat_slot, mode="drop")
    )
    token_row = slot_of_row // TOPK
    send_x = gathered_x[token_row]
    send_dy = gathered_dy[token_row]
    weight = (gate_int.reshape(-1).astype(jnp.float32) / 1024.0).astype(jnp.bfloat16)
    send_gate = weight[slot_of_row]

    recv_x = lax.all_to_all(
        send_x.reshape(n_local, per_dest, model_width), "local", 0, 0, tiled=True
    )
    recv_dy = lax.all_to_all(
        send_dy.reshape(n_local, per_dest, model_width), "local", 0, 0, tiled=True
    )
    recv_gate = lax.all_to_all(send_gate.reshape(n_local, per_dest), "local", 0, 0, tiled=True)

    saved = (
        gate_saved.reshape(n_node, n_local, capacity, FF)
        .transpose(1, 0, 2, 3)
        .reshape(row_count, FF)
    )
    contrib = expert_backward(
        recv_x.reshape(row_count, model_width),
        recv_dy.reshape(row_count, model_width),
        recv_gate.reshape(row_count),
        saved,
        w_in[0],
        w_out[0],
    )
    returned = lax.all_to_all(
        contrib.reshape(n_local, per_dest, model_width), "local", 0, 0, tiled=True
    ).reshape(row_count, model_width)

    token_pos = position.reshape(n_node * tok, TOPK)
    first = jnp.min(token_pos, axis=1)
    second = jnp.max(jnp.where(token_pos < row_count, token_pos, -1), axis=1)
    has_pair = first < row_count
    first = jnp.where(has_pair, first, 0)
    second = jnp.where(has_pair, second, 0)
    pair = returned[first].astype(jnp.float32) + returned[second].astype(jnp.float32)
    node_sum = jnp.where(has_pair[:, None], pair, 0.0).astype(jnp.bfloat16)

    back = lax.all_to_all(
        node_sum.reshape(n_node, tok, model_width), "node", 0, 0, tiled=True
    )
    return jnp.sum(back.astype(jnp.float32), axis=0).astype(jnp.bfloat16)


def solution(mesh):
    in_specs = (
        P(("node", "local"), None),
        P(("node", "local"), None),
        P(None, "local", None),
        P(None, "local", None),
        P(("node", "local"), None),
        P(("node", "local"), None, None),
        P(("node", "local"), None, None),
    )
    out_specs = P(("node", "local"), None)
    return jax.shard_map(
        on_device, mesh=mesh, in_specs=in_specs, out_specs=out_specs, check_vma=False
    )
```

```python
import jax
import jax.numpy as jnp
from jax import lax
from jax.sharding import PartitionSpec as P

FF = 1024
TOK_DEV = 128
TOPK = 8


def slot_ranks(ids, columns):
    slots = ids.shape[-1]
    onehot = (ids[..., None] == jnp.arange(columns, dtype=jnp.int32)).astype(jnp.bfloat16)
    order = jnp.arange(slots, dtype=jnp.int32)
    earlier = (order[:, None] > order[None, :]).astype(jnp.bfloat16)
    before = jnp.einsum("st,nte->nse", earlier, onehot, preferred_element_type=jnp.float32)
    return jnp.sum(before * onehot.astype(jnp.float32), axis=-1).astype(jnp.int32)


def line_gather(block, n_node, node_here):
    gathered = jnp.zeros((n_node,) + block.shape, block.dtype)
    gathered = lax.dynamic_update_slice_in_dim(gathered, block[None], node_here, 0)
    from_low = block
    from_high = block
    for hop in range(1, n_node):
        up = [(i, i + 1) for i in range(hop - 1, n_node - 1)]
        down = [(i, i - 1) for i in range(1, n_node - hop + 1)]
        from_low = lax.ppermute(from_low, "node", up)
        from_high = lax.ppermute(from_high, "node", down)
        for held, source, valid in (
            (from_low, node_here - hop, node_here >= hop),
            (from_high, node_here + hop, node_here + hop < n_node),
        ):
            index = jnp.clip(source, 0, n_node - 1)
            current = lax.dynamic_index_in_dim(gathered, index, 0, keepdims=True)
            gathered = lax.dynamic_update_slice_in_dim(
                gathered, jnp.where(valid, held[None], current), index, 0
            )
    return gathered.reshape((n_node * block.shape[0],) + block.shape[1:])


def expert_backward(rows_x, rows_dy, rows_gate, saved, weight_in, weight_out):
    up_pre = jnp.dot(rows_x, weight_in[:, FF:], preferred_element_type=jnp.float32)
    grad_hidden = lax.dot_general(
        rows_dy, weight_out, (((1,), (1,)), ((), ())), preferred_element_type=jnp.float32
    )
    grad_hidden = grad_hidden * rows_gate.astype(jnp.float32)[:, None]
    gate_pre = saved.astype(jnp.float32)
    sigmoid_gate = jax.nn.sigmoid(gate_pre)
    grad_gate = grad_hidden * up_pre * sigmoid_gate * (1.0 + gate_pre * (1.0 - sigmoid_gate))
    grad_up = grad_hidden * gate_pre * sigmoid_gate
    grad_pre = jnp.concatenate([grad_gate, grad_up], axis=1).astype(jnp.bfloat16)
    contrib = lax.dot_general(
        grad_pre, weight_in, (((1,), (1,)), ((), ())), preferred_element_type=jnp.float32
    )
    return contrib.astype(jnp.bfloat16)


def select_rows(onehot, rows):
    picked = lax.dot_general(
        onehot, rows, (((0,), (0,)), ((), ())), preferred_element_type=jnp.float32
    )
    return picked.astype(jnp.bfloat16)


def on_device(hidden_in, out_grad, expert_ids, gate_int, gate_saved, w_in, w_out):
    n_node = lax.axis_size("node")
    n_local = lax.axis_size("local")
    experts = n_node * n_local
    tok = hidden_in.shape[0]
    capacity = tok * TOPK // experts
    per_dest = n_node * capacity
    row_count = n_local * per_dest
    model_width = hidden_in.shape[1]
    node_here = lax.axis_index("node")

    gathered_x = line_gather(hidden_in, n_node, node_here)
    gathered_dy = line_gather(out_grad, n_node, node_here)

    ids = expert_ids.reshape(n_node, tok * TOPK)
    ranks = slot_ranks(ids, experts)
    on_here = (ids // n_local) == node_here
    node_range = jnp.arange(n_node, dtype=jnp.int32)[:, None]
    position = (ids % n_local) * per_dest + node_range * capacity + ranks
    position = jnp.where(on_here, position, row_count)
    slot_hits = (
        position.reshape(n_node * tok, TOPK)[:, :, None]
        == jnp.arange(row_count, dtype=jnp.int32)[None, None, :]
    ).astype(jnp.bfloat16)
    dispatch = jnp.sum(slot_hits, axis=1)
    weight = (gate_int.reshape(n_node * tok, TOPK).astype(jnp.float32) / 1024.0).astype(
        jnp.bfloat16
    )
    send_gate = jnp.einsum(
        "tk,tkr->r", weight, slot_hits, preferred_element_type=jnp.float32
    ).astype(jnp.bfloat16)

    send_x = select_rows(dispatch, gathered_x)
    recv_x = lax.all_to_all(
        send_x.reshape(n_local, per_dest, model_width), "local", 0, 0, tiled=True
    )
    send_dy = select_rows(dispatch, gathered_dy)
    recv_dy = lax.all_to_all(
        send_dy.reshape(n_local, per_dest, model_width), "local", 0, 0, tiled=True
    )
    recv_gate = lax.all_to_all(send_gate.reshape(n_local, per_dest), "local", 0, 0, tiled=True)

    saved = (
        gate_saved.reshape(n_node, n_local, capacity, FF)
        .transpose(1, 0, 2, 3)
        .reshape(row_count, FF)
    )
    contrib = expert_backward(
        recv_x.reshape(row_count, model_width),
        recv_dy.reshape(row_count, model_width),
        recv_gate.reshape(row_count),
        saved,
        w_in[0],
        w_out[0],
    )
    returned = lax.all_to_all(
        contrib.reshape(n_local, per_dest, model_width), "local", 0, 0, tiled=True
    ).reshape(row_count, model_width)

    node_sum = jnp.dot(dispatch, returned, preferred_element_type=jnp.float32).astype(
        jnp.bfloat16
    )

    back = lax.all_to_all(
        node_sum.reshape(n_node, tok, model_width), "node", 0, 0, tiled=True
    )
    return jnp.sum(back.astype(jnp.float32), axis=0).astype(jnp.bfloat16)


def solution(mesh):
    in_specs = (
        P(("node", "local"), None),
        P(("node", "local"), None),
        P(None, "local", None),
        P(None, "local", None),
        P(("node", "local"), None),
        P(("node", "local"), None, None),
        P(("node", "local"), None, None),
    )
    out_specs = P(("node", "local"), None)
    return jax.shard_map(
        on_device, mesh=mesh, in_specs=in_specs, out_specs=out_specs, check_vma=False
    )
```

```python
import jax
import jax.numpy as jnp
from jax import lax
from jax.sharding import PartitionSpec as P

FF = 1024
TOK_DEV = 128
TOPK = 8


def slot_ranks(ids, columns):
    slots = ids.shape[-1]
    onehot = (ids[..., None] == jnp.arange(columns, dtype=jnp.int32)).astype(jnp.bfloat16)
    order = jnp.arange(slots, dtype=jnp.int32)
    earlier = (order[:, None] > order[None, :]).astype(jnp.bfloat16)
    before = jnp.einsum("st,nte->nse", earlier, onehot, preferred_element_type=jnp.float32)
    return jnp.sum(before * onehot.astype(jnp.float32), axis=-1).astype(jnp.int32)


def expert_backward(rows_x, rows_dy, rows_gate, saved, weight_in, weight_out):
    up_pre = jnp.dot(rows_x, weight_in[:, FF:], preferred_element_type=jnp.float32)
    grad_hidden = lax.dot_general(
        rows_dy, weight_out, (((1,), (1,)), ((), ())), preferred_element_type=jnp.float32
    )
    grad_hidden = grad_hidden * rows_gate.astype(jnp.float32)[:, None]
    gate_pre = saved.astype(jnp.float32)
    sigmoid_gate = jax.nn.sigmoid(gate_pre)
    grad_gate = grad_hidden * up_pre * sigmoid_gate * (1.0 + gate_pre * (1.0 - sigmoid_gate))
    grad_up = grad_hidden * gate_pre * sigmoid_gate
    grad_pre = jnp.concatenate([grad_gate, grad_up], axis=1).astype(jnp.bfloat16)
    contrib = lax.dot_general(
        grad_pre, weight_in, (((1,), (1,)), ((), ())), preferred_element_type=jnp.float32
    )
    return contrib.astype(jnp.bfloat16)


def select_rows(onehot, rows):
    picked = lax.dot_general(
        onehot, rows, (((0,), (0,)), ((), ())), preferred_element_type=jnp.float32
    )
    return picked.astype(jnp.bfloat16)


def shift(value, n_node, step):
    if step % n_node == 0:
        return value
    return lax.ppermute(value, "node", [(i, (i + step) % n_node) for i in range(n_node)])


def on_device(hidden_in, out_grad, expert_ids, gate_int, gate_saved, w_in, w_out):
    n_node = lax.axis_size("node")
    n_local = lax.axis_size("local")
    experts = n_node * n_local
    tok = hidden_in.shape[0]
    capacity = tok * TOPK // experts
    chunk_rows = n_local * capacity
    model_width = hidden_in.shape[1]
    node_here = lax.axis_index("node")
    weight_in = w_in[0]
    weight_out = w_out[0]

    ids = expert_ids.reshape(n_node, tok * TOPK)
    ranks = slot_ranks(ids, experts)
    on_here = (ids // n_local) == node_here
    position = jnp.where(on_here, (ids % n_local) * capacity + ranks, chunk_rows)
    weight = (gate_int.reshape(n_node, tok, TOPK).astype(jnp.float32) / 1024.0).astype(
        jnp.bfloat16
    )
    row_range = jnp.arange(chunk_rows, dtype=jnp.int32)

    total = None
    for step in range(n_node):
        source = (node_here - step) % n_node
        chunk_x = shift(hidden_in, n_node, step)
        chunk_dy = shift(out_grad, n_node, step)
        chunk_pos = lax.dynamic_index_in_dim(position, source, 0, keepdims=False)
        hits = (
            chunk_pos.reshape(tok, TOPK)[:, :, None] == row_range[None, None, :]
        ).astype(jnp.bfloat16)
        dispatch = jnp.sum(hits, axis=1)
        chunk_weight = lax.dynamic_index_in_dim(weight, source, 0, keepdims=False)
        send_gate = jnp.einsum(
            "tk,tkr->r", chunk_weight, hits, preferred_element_type=jnp.float32
        ).astype(jnp.bfloat16)

        recv_x = lax.all_to_all(
            select_rows(dispatch, chunk_x).reshape(n_local, capacity, model_width),
            "local", 0, 0, tiled=True,
        )
        recv_dy = lax.all_to_all(
            select_rows(dispatch, chunk_dy).reshape(n_local, capacity, model_width),
            "local", 0, 0, tiled=True,
        )
        recv_gate = lax.all_to_all(
            send_gate.reshape(n_local, capacity), "local", 0, 0, tiled=True
        )
        saved = lax.dynamic_slice_in_dim(gate_saved, source * chunk_rows, chunk_rows, 0)
        contrib = expert_backward(
            recv_x.reshape(chunk_rows, model_width),
            recv_dy.reshape(chunk_rows, model_width),
            recv_gate.reshape(chunk_rows),
            saved,
            weight_in,
            weight_out,
        )
        returned = lax.all_to_all(
            contrib.reshape(n_local, capacity, model_width), "local", 0, 0, tiled=True
        ).reshape(chunk_rows, model_width)
        node_sum = jnp.dot(dispatch, returned, preferred_element_type=jnp.float32).astype(
            jnp.bfloat16
        )
        home = shift(node_sum, n_node, -step).astype(jnp.float32)
        total = home if total is None else total + home
    return total.astype(jnp.bfloat16)


def solution(mesh):
    in_specs = (
        P(("node", "local"), None),
        P(("node", "local"), None),
        P(None, "local", None),
        P(None, "local", None),
        P(("node", "local"), None),
        P(("node", "local"), None, None),
        P(("node", "local"), None, None),
    )
    out_specs = P(("node", "local"), None)
    return jax.shard_map(
        on_device, mesh=mesh, in_specs=in_specs, out_specs=out_specs, check_vma=False
    )
```

```python
import jax
import jax.numpy as jnp
from jax import lax
from jax.sharding import PartitionSpec as P

FF = 1024
TOK_DEV = 128
TOPK = 8


def slot_ranks(ids, columns):
    slots = ids.shape[-1]
    onehot = (ids[..., None] == jnp.arange(columns, dtype=jnp.int32)).astype(jnp.bfloat16)
    order = jnp.arange(slots, dtype=jnp.int32)
    earlier = (order[:, None] > order[None, :]).astype(jnp.bfloat16)
    before = jnp.einsum("st,nte->nse", earlier, onehot, preferred_element_type=jnp.float32)
    return jnp.sum(before * onehot.astype(jnp.float32), axis=-1).astype(jnp.int32)


def expert_backward(rows_x, rows_dy, rows_gate, saved, weight_in, weight_out):
    up_pre = jnp.dot(rows_x, weight_in[:, FF:], preferred_element_type=jnp.float32)
    grad_hidden = lax.dot_general(
        rows_dy, weight_out, (((1,), (1,)), ((), ())), preferred_element_type=jnp.float32
    )
    grad_hidden = grad_hidden * rows_gate.astype(jnp.float32)[:, None]
    gate_pre = saved.astype(jnp.float32)
    sigmoid_gate = jax.nn.sigmoid(gate_pre)
    grad_gate = grad_hidden * up_pre * sigmoid_gate * (1.0 + gate_pre * (1.0 - sigmoid_gate))
    grad_up = grad_hidden * gate_pre * sigmoid_gate
    grad_pre = jnp.concatenate([grad_gate, grad_up], axis=1).astype(jnp.bfloat16)
    contrib = lax.dot_general(
        grad_pre, weight_in, (((1,), (1,)), ((), ())), preferred_element_type=jnp.float32
    )
    return contrib.astype(jnp.bfloat16)


def select_rows(onehot, rows):
    picked = lax.dot_general(
        onehot, rows, (((0,), (0,)), ((), ())), preferred_element_type=jnp.float32
    )
    return picked.astype(jnp.bfloat16)


def shift(value, n_node, step):
    if step % n_node == 0:
        return value
    return lax.ppermute(value, "node", [(i, (i + step) % n_node) for i in range(n_node)])


def on_device(hidden_in, out_grad, expert_ids, gate_int, gate_saved, w_in, w_out):
    n_node = lax.axis_size("node")
    n_local = lax.axis_size("local")
    experts = n_node * n_local
    tok = hidden_in.shape[0]
    capacity = tok * TOPK // experts
    chunk_rows = n_local * capacity
    model_width = hidden_in.shape[1]
    node_here = lax.axis_index("node")
    weight_in = w_in[0]
    weight_out = w_out[0]

    ids = expert_ids.reshape(n_node, tok * TOPK)
    ranks = slot_ranks(ids, experts)
    on_here = (ids // n_local) == node_here
    position = jnp.where(on_here, (ids % n_local) * capacity + ranks, chunk_rows)
    weight = (gate_int.reshape(n_node, tok, TOPK).astype(jnp.float32) / 1024.0).astype(
        jnp.bfloat16
    )
    row_range = jnp.arange(chunk_rows, dtype=jnp.int32)

    sources = [(node_here - step) % n_node for step in range(n_node)]
    dispatch = []
    send_gate = []
    for step in range(n_node):
        chunk_pos = lax.dynamic_index_in_dim(position, sources[step], 0, keepdims=False)
        hits = (
            chunk_pos.reshape(tok, TOPK)[:, :, None] == row_range[None, None, :]
        ).astype(jnp.bfloat16)
        dispatch.append(jnp.sum(hits, axis=1))
        chunk_weight = lax.dynamic_index_in_dim(weight, sources[step], 0, keepdims=False)
        send_gate.append(
            jnp.einsum("tk,tkr->r", chunk_weight, hits, preferred_element_type=jnp.float32)
            .astype(jnp.bfloat16)
            .reshape(n_local, capacity)
        )

    def spread(rows):
        return lax.all_to_all(
            rows.reshape(n_local, capacity, model_width), "local", 0, 0, tiled=True
        )

    def fetch(step, previous):
        return shift(previous[0], n_node, 1), shift(previous[1], n_node, 1)

    def send(step, chunk):
        return (
            spread(select_rows(dispatch[step], chunk[0])),
            spread(select_rows(dispatch[step], chunk[1])),
            lax.all_to_all(send_gate[step], "local", 0, 0, tiled=True),
        )

    def compute(step, received):
        saved = lax.dynamic_slice_in_dim(gate_saved, sources[step] * chunk_rows, chunk_rows, 0)
        return expert_backward(
            received[0].reshape(chunk_rows, model_width),
            received[1].reshape(chunk_rows, model_width),
            received[2].reshape(chunk_rows),
            saved,
            weight_in,
            weight_out,
        )

    def gather_back(step, contrib):
        returned = spread(contrib).reshape(chunk_rows, model_width)
        return jnp.dot(dispatch[step], returned, preferred_element_type=jnp.float32).astype(
            jnp.bfloat16
        )

    def send_home(step, node_sum):
        return shift(node_sum, n_node, -step)

    chunks = {0: (hidden_in, out_grad)}
    received = {}
    contribs = {}
    sums = {}
    homes = {}
    for slot in range(-1, n_node + 2):
        produced = {}
        if 0 < slot + 2 < n_node:
            produced["chunk", slot + 2] = fetch(slot + 2, chunks[slot + 1])
        if 0 <= slot + 1 < n_node:
            produced["received", slot + 1] = send(slot + 1, chunks[slot + 1])
        if 0 <= slot < n_node:
            produced["contrib", slot] = compute(slot, received[slot])
        if 0 <= slot - 1 < n_node:
            produced["sum", slot - 1] = gather_back(slot - 1, contribs[slot - 1])
        if 0 <= slot - 2 < n_node:
            produced["home", slot - 2] = send_home(slot - 2, sums[slot - 2])
        keys = list(produced)
        values = lax.optimization_barrier([produced[key] for key in keys])
        for (kind, step), value in zip(keys, values):
            {"chunk": chunks, "received": received, "contrib": contribs, "sum": sums,
             "home": homes}[kind][step] = value

    total = homes[0].astype(jnp.float32)
    for step in range(1, n_node):
        total = total + homes[step].astype(jnp.float32)
    return total.astype(jnp.bfloat16)


def solution(mesh):
    in_specs = (
        P(("node", "local"), None),
        P(("node", "local"), None),
        P(None, "local", None),
        P(None, "local", None),
        P(("node", "local"), None),
        P(("node", "local"), None, None),
        P(("node", "local"), None, None),
    )
    out_specs = P(("node", "local"), None)
    return jax.shard_map(
        on_device, mesh=mesh, in_specs=in_specs, out_specs=out_specs, check_vma=False
    )
```

```python
import jax
import jax.numpy as jnp
from jax import lax
from jax.sharding import PartitionSpec as P

FF = 1024
TOK_DEV = 128
TOPK = 8


def slot_ranks(ids, columns):
    slots = ids.shape[-1]
    onehot = (ids[..., None] == jnp.arange(columns, dtype=jnp.int32)).astype(jnp.bfloat16)
    order = jnp.arange(slots, dtype=jnp.int32)
    earlier = (order[:, None] > order[None, :]).astype(jnp.bfloat16)
    before = jnp.einsum("st,nte->nse", earlier, onehot, preferred_element_type=jnp.float32)
    return jnp.sum(before * onehot.astype(jnp.float32), axis=-1).astype(jnp.int32)


def expert_backward(rows_x, rows_dy, rows_gate, saved, weight_in, weight_out):
    up_pre = jnp.dot(rows_x, weight_in[:, FF:], preferred_element_type=jnp.float32)
    grad_hidden = lax.dot_general(
        rows_dy, weight_out, (((1,), (1,)), ((), ())), preferred_element_type=jnp.float32
    )
    grad_hidden = grad_hidden * rows_gate.astype(jnp.float32)[:, None]
    gate_pre = saved.astype(jnp.float32)
    sigmoid_gate = jax.nn.sigmoid(gate_pre)
    grad_gate = grad_hidden * up_pre * sigmoid_gate * (1.0 + gate_pre * (1.0 - sigmoid_gate))
    grad_up = grad_hidden * gate_pre * sigmoid_gate
    grad_pre = jnp.concatenate([grad_gate, grad_up], axis=1).astype(jnp.bfloat16)
    contrib = lax.dot_general(
        grad_pre, weight_in, (((1,), (1,)), ((), ())), preferred_element_type=jnp.float32
    )
    return contrib.astype(jnp.bfloat16)


def select_rows(onehot, rows):
    picked = lax.dot_general(
        onehot, rows, (((0,), (0,)), ((), ())), preferred_element_type=jnp.float32
    )
    return picked.astype(jnp.bfloat16)


def shift(value, n_node, step):
    if step % n_node == 0:
        return value
    return lax.ppermute(value, "node", [(i, (i + step) % n_node) for i in range(n_node)])


def on_device(hidden_in, out_grad, expert_ids, gate_int, gate_saved, w_in, w_out):
    n_node = lax.axis_size("node")
    n_local = lax.axis_size("local")
    experts = n_node * n_local
    tok = hidden_in.shape[0]
    capacity = tok * TOPK // experts
    chunk_rows = n_local * capacity
    model_width = hidden_in.shape[1]
    node_here = lax.axis_index("node")
    weight_in = w_in[0]
    weight_out = w_out[0]

    ids = expert_ids.reshape(n_node, tok * TOPK)
    ranks = slot_ranks(ids, experts)
    on_here = (ids // n_local) == node_here
    position = jnp.where(on_here, (ids % n_local) * capacity + ranks, chunk_rows)
    weight = (gate_int.reshape(n_node, tok, TOPK).astype(jnp.float32) / 1024.0).astype(
        jnp.bfloat16
    )
    row_range = jnp.arange(chunk_rows, dtype=jnp.int32)

    sources = [(node_here - step) % n_node for step in range(n_node)]
    dispatch = []
    send_gate = []
    for step in range(n_node):
        chunk_pos = lax.dynamic_index_in_dim(position, sources[step], 0, keepdims=False)
        hits = (
            chunk_pos.reshape(tok, TOPK)[:, :, None] == row_range[None, None, :]
        ).astype(jnp.bfloat16)
        dispatch.append(jnp.sum(hits, axis=1))
        chunk_weight = lax.dynamic_index_in_dim(weight, sources[step], 0, keepdims=False)
        send_gate.append(
            jnp.einsum("tk,tkr->r", chunk_weight, hits, preferred_element_type=jnp.float32)
            .astype(jnp.bfloat16)
            .reshape(n_local, capacity)
        )
    gates = lax.all_to_all(jnp.stack(send_gate, axis=1), "local", 0, 0, tiled=True)

    def spread(rows):
        return lax.all_to_all(
            rows.reshape(n_local, capacity, rows.shape[-1]), "local", 0, 0, tiled=True
        )

    def fetch(step, previous):
        return shift(previous, n_node, 1)

    def send(step, chunk):
        return spread(select_rows(dispatch[step], chunk))

    def compute(step, received):
        saved = lax.dynamic_slice_in_dim(gate_saved, sources[step] * chunk_rows, chunk_rows, 0)
        rows = received.reshape(chunk_rows, 2 * model_width)
        return expert_backward(
            rows[:, :model_width],
            rows[:, model_width:],
            gates[:, step].reshape(chunk_rows),
            saved,
            weight_in,
            weight_out,
        )

    def gather_back(step, contrib):
        returned = spread(contrib).reshape(chunk_rows, model_width)
        return jnp.dot(dispatch[step], returned, preferred_element_type=jnp.float32).astype(
            jnp.bfloat16
        )

    def send_home(step, node_sum):
        return shift(node_sum, n_node, -step)

    chunks = {0: jnp.concatenate([hidden_in, out_grad], axis=1)}
    received = {}
    contribs = {}
    sums = {}
    homes = {}
    for slot in range(-1, n_node + 2):
        produced = {}
        if 0 < slot + 2 < n_node:
            produced["chunk", slot + 2] = fetch(slot + 2, chunks[slot + 1])
        if 0 <= slot + 1 < n_node:
            produced["received", slot + 1] = send(slot + 1, chunks[slot + 1])
        if 0 <= slot < n_node:
            produced["contrib", slot] = compute(slot, received[slot])
        if 0 <= slot - 1 < n_node:
            produced["sum", slot - 1] = gather_back(slot - 1, contribs[slot - 1])
        if 0 <= slot - 2 < n_node:
            produced["home", slot - 2] = send_home(slot - 2, sums[slot - 2])
        keys = list(produced)
        values = lax.optimization_barrier([produced[key] for key in keys])
        for (kind, step), value in zip(keys, values):
            {"chunk": chunks, "received": received, "contrib": contribs, "sum": sums,
             "home": homes}[kind][step] = value

    total = homes[0].astype(jnp.float32)
    for step in range(1, n_node):
        total = total + homes[step].astype(jnp.float32)
    return total.astype(jnp.bfloat16)


def solution(mesh):
    in_specs = (
        P(("node", "local"), None),
        P(("node", "local"), None),
        P(None, "local", None),
        P(None, "local", None),
        P(("node", "local"), None),
        P(("node", "local"), None, None),
        P(("node", "local"), None, None),
    )
    out_specs = P(("node", "local"), None)
    return jax.shard_map(
        on_device, mesh=mesh, in_specs=in_specs, out_specs=out_specs, check_vma=False
    )
```

```python
import jax
import jax.numpy as jnp
from jax import lax
from jax.sharding import PartitionSpec as P

FF = 1024
TOK_DEV = 128
TOPK = 8


def slot_ranks(ids, columns):
    slots = ids.shape[-1]
    onehot = (ids[..., None] == jnp.arange(columns, dtype=jnp.int32)).astype(jnp.bfloat16)
    order = jnp.arange(slots, dtype=jnp.int32)
    earlier = (order[:, None] > order[None, :]).astype(jnp.bfloat16)
    before = jnp.einsum("st,nte->nse", earlier, onehot, preferred_element_type=jnp.float32)
    return jnp.sum(before * onehot.astype(jnp.float32), axis=-1).astype(jnp.int32)


def expert_backward(rows_x, rows_dy, rows_gate, saved, weight_in, weight_out):
    up_pre = jnp.dot(rows_x, weight_in[:, FF:], preferred_element_type=jnp.float32)
    grad_hidden = lax.dot_general(
        rows_dy, weight_out, (((1,), (1,)), ((), ())), preferred_element_type=jnp.float32
    )
    grad_hidden = grad_hidden * rows_gate.astype(jnp.float32)[:, None]
    gate_pre = saved.astype(jnp.float32)
    sigmoid_gate = jax.nn.sigmoid(gate_pre)
    grad_gate = grad_hidden * up_pre * sigmoid_gate * (1.0 + gate_pre * (1.0 - sigmoid_gate))
    grad_up = grad_hidden * gate_pre * sigmoid_gate
    grad_pre = jnp.concatenate([grad_gate, grad_up], axis=1).astype(jnp.bfloat16)
    contrib = lax.dot_general(
        grad_pre, weight_in, (((1,), (1,)), ((), ())), preferred_element_type=jnp.float32
    )
    return contrib.astype(jnp.bfloat16)


def select_rows(onehot, rows):
    picked = lax.dot_general(
        onehot, rows, (((0,), (0,)), ((), ())), preferred_element_type=jnp.float32
    )
    return picked.astype(jnp.bfloat16)


def shift(value, n_node, step):
    if step % n_node == 0:
        return value
    return lax.ppermute(value, "node", [(i, (i + step) % n_node) for i in range(n_node)])


def on_device(hidden_in, out_grad, expert_ids, gate_int, gate_saved, w_in, w_out):
    n_node = lax.axis_size("node")
    n_local = lax.axis_size("local")
    experts = n_node * n_local
    tok = hidden_in.shape[0]
    capacity = tok * TOPK // experts
    chunk_rows = n_local * capacity
    model_width = hidden_in.shape[1]
    node_here = lax.axis_index("node")
    weight_in = w_in[0]
    weight_out = w_out[0]

    ids = expert_ids.reshape(n_node, tok * TOPK)
    ranks = slot_ranks(ids, experts)
    on_here = (ids // n_local) == node_here
    position = jnp.where(on_here, (ids % n_local) * capacity + ranks, chunk_rows)
    weight = (gate_int.reshape(n_node, tok, TOPK).astype(jnp.float32) / 1024.0).astype(
        jnp.bfloat16
    )
    row_range = jnp.arange(chunk_rows, dtype=jnp.int32)

    sources = [(node_here - step) % n_node for step in range(n_node)]
    dispatch = []
    send_gate = []
    for step in range(n_node):
        chunk_pos = lax.dynamic_index_in_dim(position, sources[step], 0, keepdims=False)
        hits = (
            chunk_pos.reshape(tok, TOPK)[:, :, None] == row_range[None, None, :]
        ).astype(jnp.bfloat16)
        dispatch.append(jnp.sum(hits, axis=1))
        chunk_weight = lax.dynamic_index_in_dim(weight, sources[step], 0, keepdims=False)
        send_gate.append(
            jnp.einsum("tk,tkr->r", chunk_weight, hits, preferred_element_type=jnp.float32)
            .astype(jnp.bfloat16)
            .reshape(n_local, capacity)
        )
    gates = lax.all_to_all(jnp.stack(send_gate, axis=1), "local", 0, 0, tiled=True)

    def spread(rows):
        return lax.all_to_all(
            rows.reshape(n_local, capacity, rows.shape[-1]), "local", 0, 0, tiled=True
        )

    def fetch(step, previous):
        return shift(previous, n_node, 1)

    def compute(step, received):
        saved = lax.dynamic_slice_in_dim(gate_saved, sources[step] * chunk_rows, chunk_rows, 0)
        rows = received
        return expert_backward(
            rows[:, :model_width],
            rows[:, model_width:],
            gates[:, step].reshape(chunk_rows),
            saved,
            weight_in,
            weight_out,
        )

    def send_home(step, node_sum):
        return shift(node_sum, n_node, -step)

    chunks = {0: jnp.concatenate([hidden_in, out_grad], axis=1)}
    received = {}
    contribs = {}
    homes = {}
    for slot in range(-1, n_node + 1):
        produced = {}
        if 0 < slot + 2 < n_node:
            produced["chunk", slot + 2] = fetch(slot + 2, chunks[slot + 1])
        if 0 <= slot < n_node:
            produced["contrib", slot] = compute(slot, received[slot])
        outgoing = []
        if 0 <= slot + 1 < n_node:
            outgoing.append(select_rows(dispatch[slot + 1], chunks[slot + 1]))
        if 0 <= slot - 1 < n_node:
            outgoing.append(contribs[slot - 1])
        arrived = spread(jnp.concatenate(outgoing, axis=1) if len(outgoing) > 1 else outgoing[0])
        arrived = arrived.reshape(chunk_rows, arrived.shape[-1])
        if 0 <= slot + 1 < n_node:
            produced["received", slot + 1] = arrived[:, : 2 * model_width]
        if 0 <= slot - 1 < n_node:
            returned = arrived[:, arrived.shape[-1] - model_width :]
            node_sum = jnp.dot(
                dispatch[slot - 1], returned, preferred_element_type=jnp.float32
            ).astype(jnp.bfloat16)
            produced["home", slot - 1] = send_home(slot - 1, node_sum)
        keys = list(produced)
        values = lax.optimization_barrier([produced[key] for key in keys])
        for (kind, step), value in zip(keys, values):
            {"chunk": chunks, "received": received, "contrib": contribs, "home": homes}[kind][
                step
            ] = value

    total = homes[0].astype(jnp.float32)
    for step in range(1, n_node):
        total = total + homes[step].astype(jnp.float32)
    return total.astype(jnp.bfloat16)


def solution(mesh):
    in_specs = (
        P(("node", "local"), None),
        P(("node", "local"), None),
        P(None, "local", None),
        P(None, "local", None),
        P(("node", "local"), None),
        P(("node", "local"), None, None),
        P(("node", "local"), None, None),
    )
    out_specs = P(("node", "local"), None)
    return jax.shard_map(
        on_device, mesh=mesh, in_specs=in_specs, out_specs=out_specs, check_vma=False
    )
```

```python
import jax
import jax.numpy as jnp
from jax import lax
from jax.sharding import PartitionSpec as P

FF = 1024
TOK_DEV = 128
TOPK = 8


def slot_ranks(ids, columns):
    slots = ids.shape[-1]
    onehot = (ids[..., None] == jnp.arange(columns, dtype=jnp.int32)).astype(jnp.bfloat16)
    order = jnp.arange(slots, dtype=jnp.int32)
    earlier = (order[:, None] > order[None, :]).astype(jnp.bfloat16)
    before = jnp.einsum("st,nte->nse", earlier, onehot, preferred_element_type=jnp.float32)
    return jnp.sum(before * onehot.astype(jnp.float32), axis=-1).astype(jnp.int32)


def expert_grad_pre(rows_x, rows_dy, rows_gate, saved, weight_in, weight_out):
    up_pre = jnp.dot(rows_x, weight_in[:, FF:], preferred_element_type=jnp.float32)
    grad_hidden = lax.dot_general(
        rows_dy, weight_out, (((1,), (1,)), ((), ())), preferred_element_type=jnp.float32
    )
    grad_hidden = grad_hidden * rows_gate.astype(jnp.float32)[:, None]
    gate_pre = saved.astype(jnp.float32)
    sigmoid_gate = jax.nn.sigmoid(gate_pre)
    grad_gate = grad_hidden * up_pre * sigmoid_gate * (1.0 + gate_pre * (1.0 - sigmoid_gate))
    grad_up = grad_hidden * gate_pre * sigmoid_gate
    return jnp.concatenate([grad_gate, grad_up], axis=1).astype(jnp.bfloat16)


def expert_part(grad_pre, weight_in):
    contrib = lax.dot_general(
        grad_pre, weight_in, (((1,), (1,)), ((), ())), preferred_element_type=jnp.float32
    )
    return contrib.astype(jnp.bfloat16)


def select_rows(onehot, rows):
    picked = lax.dot_general(
        onehot, rows, (((0,), (0,)), ((), ())), preferred_element_type=jnp.float32
    )
    return picked.astype(jnp.bfloat16)


def shift(value, n_node, step):
    if step % n_node == 0:
        return value
    return lax.ppermute(value, "node", [(i, (i + step) % n_node) for i in range(n_node)])


def on_device(hidden_in, out_grad, expert_ids, gate_int, gate_saved, w_in, w_out):
    n_node = lax.axis_size("node")
    n_local = lax.axis_size("local")
    experts = n_node * n_local
    tok = hidden_in.shape[0]
    capacity = tok * TOPK // experts
    chunk_rows = n_local * capacity
    model_width = hidden_in.shape[1]
    node_here = lax.axis_index("node")
    weight_in = w_in[0]
    weight_out = w_out[0]

    ids = expert_ids.reshape(n_node, tok * TOPK)
    ranks = slot_ranks(ids, experts)
    on_here = (ids // n_local) == node_here
    position = jnp.where(on_here, (ids % n_local) * capacity + ranks, chunk_rows)
    weight = (gate_int.reshape(n_node, tok, TOPK).astype(jnp.float32) / 1024.0).astype(
        jnp.bfloat16
    )
    row_range = jnp.arange(chunk_rows, dtype=jnp.int32)

    sources = [(node_here - step) % n_node for step in range(n_node)]
    dispatch = []
    send_gate = []
    for step in range(n_node):
        chunk_pos = lax.dynamic_index_in_dim(position, sources[step], 0, keepdims=False)
        hits = (
            chunk_pos.reshape(tok, TOPK)[:, :, None] == row_range[None, None, :]
        ).astype(jnp.bfloat16)
        dispatch.append(jnp.sum(hits, axis=1))
        chunk_weight = lax.dynamic_index_in_dim(weight, sources[step], 0, keepdims=False)
        send_gate.append(
            jnp.einsum("tk,tkr->r", chunk_weight, hits, preferred_element_type=jnp.float32)
            .astype(jnp.bfloat16)
            .reshape(n_local, capacity)
        )
    gates = lax.all_to_all(jnp.stack(send_gate, axis=1), "local", 0, 0, tiled=True)

    def spread(rows):
        return lax.all_to_all(
            rows.reshape(n_local, capacity, rows.shape[-1]), "local", 0, 0, tiled=True
        )

    def fetch(step, previous):
        return shift(previous, n_node, 1)

    def send(step, chunk):
        return spread(select_rows(dispatch[step], chunk))

    def compute(step, received):
        saved = lax.dynamic_slice_in_dim(gate_saved, sources[step] * chunk_rows, chunk_rows, 0)
        rows = received.reshape(chunk_rows, 2 * model_width)
        return expert_grad_pre(
            rows[:, :model_width],
            rows[:, model_width:],
            gates[:, step].reshape(chunk_rows),
            saved,
            weight_in,
            weight_out,
        )

    def gather_back(step, contrib):
        returned = spread(contrib).reshape(chunk_rows, model_width)
        return jnp.dot(dispatch[step], returned, preferred_element_type=jnp.float32).astype(
            jnp.bfloat16
        )

    def send_home(step, node_sum):
        return shift(node_sum, n_node, -step)

    chunks = {0: jnp.concatenate([hidden_in, out_grad], axis=1)}
    received = {}
    grads = {}
    contribs = {}
    homes = {}
    stores = {"chunk": chunks, "received": received, "grad": grads, "contrib": contribs,
              "home": homes}

    def settle(produced):
        keys = list(produced)
        values = lax.optimization_barrier([produced[key] for key in keys])
        for (kind, step), value in zip(keys, values):
            stores[kind][step] = value

    carried = {}
    for slot in range(-1, n_node + 1):
        first = dict(carried)
        fetched = {}
        if 0 < slot + 2 < n_node:
            fetched["chunk", slot + 2] = fetch(slot + 2, chunks[slot + 1])
        if 0 <= slot + 1 < n_node:
            first["received", slot + 1] = send(slot + 1, chunks[slot + 1])
        if 0 <= slot < n_node:
            first["grad", slot] = compute(slot, received[slot])
        if first:
            settle(first)
        second = dict(fetched)
        carried = {}
        if 0 <= slot < n_node:
            second["contrib", slot] = expert_part(grads[slot], weight_in)
        if 0 <= slot - 1 < n_node:
            carried["home", slot - 1] = send_home(slot - 1, gather_back(slot - 1, contribs[slot - 1]))
        if second:
            settle(second)
    settle(carried)

    total = homes[0].astype(jnp.float32)
    for step in range(1, n_node):
        total = total + homes[step].astype(jnp.float32)
    return total.astype(jnp.bfloat16)


def solution(mesh):
    in_specs = (
        P(("node", "local"), None),
        P(("node", "local"), None),
        P(None, "local", None),
        P(None, "local", None),
        P(("node", "local"), None),
        P(("node", "local"), None, None),
        P(("node", "local"), None, None),
    )
    out_specs = P(("node", "local"), None)
    return jax.shard_map(
        on_device, mesh=mesh, in_specs=in_specs, out_specs=out_specs, check_vma=False
    )
```

```python
import jax
import jax.numpy as jnp
from jax import lax
from jax.sharding import PartitionSpec as P

FF = 1024
TOK_DEV = 128
TOPK = 8


def slot_ranks(ids, columns):
    slots = ids.shape[-1]
    onehot = (ids[..., None] == jnp.arange(columns, dtype=jnp.int32)).astype(jnp.bfloat16)
    order = jnp.arange(slots, dtype=jnp.int32)
    earlier = (order[:, None] > order[None, :]).astype(jnp.bfloat16)
    before = jnp.einsum("st,nte->nse", earlier, onehot, preferred_element_type=jnp.float32)
    return jnp.sum(before * onehot.astype(jnp.float32), axis=-1).astype(jnp.int32)


def expert_backward(rows_x, rows_dy, rows_gate, saved, weight_in, weight_out):
    up_pre = jnp.dot(rows_x, weight_in[:, FF:], preferred_element_type=jnp.float32)
    grad_hidden = lax.dot_general(
        rows_dy, weight_out, (((1,), (1,)), ((), ())), preferred_element_type=jnp.float32
    )
    grad_hidden = grad_hidden * rows_gate.astype(jnp.float32)[:, None]
    gate_pre = saved.astype(jnp.float32)
    sigmoid_gate = jax.nn.sigmoid(gate_pre)
    grad_gate = grad_hidden * up_pre * sigmoid_gate * (1.0 + gate_pre * (1.0 - sigmoid_gate))
    grad_up = grad_hidden * gate_pre * sigmoid_gate
    grad_pre = jnp.concatenate([grad_gate, grad_up], axis=1).astype(jnp.bfloat16)
    contrib = lax.dot_general(
        grad_pre, weight_in, (((1,), (1,)), ((), ())), preferred_element_type=jnp.float32
    )
    return contrib.astype(jnp.bfloat16)


def select_rows(onehot, rows):
    picked = lax.dot_general(
        onehot, rows, (((0,), (0,)), ((), ())), preferred_element_type=jnp.float32
    )
    return picked.astype(jnp.bfloat16)


def shift(value, n_node, step):
    if step % n_node == 0:
        return value
    return lax.ppermute(value, "node", [(i, (i + step) % n_node) for i in range(n_node)])


def on_device(hidden_in, out_grad, expert_ids, gate_int, gate_saved, w_in, w_out):
    n_node = lax.axis_size("node")
    n_local = lax.axis_size("local")
    experts = n_node * n_local
    tok = hidden_in.shape[0]
    capacity = tok * TOPK // experts
    chunk_rows = n_local * capacity
    model_width = hidden_in.shape[1]
    node_here = lax.axis_index("node")
    weight_in = w_in[0]
    weight_out = w_out[0]

    ids = expert_ids.reshape(n_node, tok * TOPK)
    ranks = slot_ranks(ids, experts)
    on_here = (ids // n_local) == node_here
    position = jnp.where(on_here, (ids % n_local) * capacity + ranks, chunk_rows)
    weight = (gate_int.reshape(n_node, tok, TOPK).astype(jnp.float32) / 1024.0).astype(
        jnp.bfloat16
    )
    row_range = jnp.arange(chunk_rows, dtype=jnp.int32)

    sources = [(node_here - step) % n_node for step in range(n_node)]
    dispatch = []
    send_gate = []
    for step in range(n_node):
        chunk_pos = lax.dynamic_index_in_dim(position, sources[step], 0, keepdims=False)
        hits = (
            chunk_pos.reshape(tok, TOPK)[:, :, None] == row_range[None, None, :]
        ).astype(jnp.bfloat16)
        dispatch.append(jnp.sum(hits, axis=1))
        chunk_weight = lax.dynamic_index_in_dim(weight, sources[step], 0, keepdims=False)
        send_gate.append(
            jnp.einsum("tk,tkr->r", chunk_weight, hits, preferred_element_type=jnp.float32)
            .astype(jnp.bfloat16)
            .reshape(n_local, capacity)
        )
    gates = lax.all_to_all(jnp.stack(send_gate, axis=1), "local", 0, 0, tiled=True)

    def spread(rows):
        return lax.all_to_all(
            rows.reshape(n_local, capacity, rows.shape[-1]), "local", 0, 0, tiled=True
        )

    def fetch(step, previous):
        return shift(previous, n_node, 1)

    def send(step, chunk):
        return spread(select_rows(dispatch[step], chunk))

    def compute(step, received):
        saved = lax.dynamic_slice_in_dim(gate_saved, sources[step] * chunk_rows, chunk_rows, 0)
        rows = received.reshape(chunk_rows, 2 * model_width)
        return expert_backward(
            rows[:, :model_width],
            rows[:, model_width:],
            gates[:, step].reshape(chunk_rows),
            saved,
            weight_in,
            weight_out,
        )

    local_here = lax.axis_index("local")

    def gather_back(step, contrib):
        blocks = contrib.reshape(n_local, capacity, model_width)
        total_sum = None
        for offset in range(n_local):
            target = (local_here + offset) % n_local
            piece = lax.dynamic_index_in_dim(blocks, target, 0, keepdims=False)
            if offset:
                piece = lax.ppermute(
                    piece, "local", [(i, (i + offset) % n_local) for i in range(n_local)]
                )
            origin = (local_here - offset) % n_local
            columns = lax.dynamic_slice_in_dim(dispatch[step], origin * capacity, capacity, 1)
            part = jnp.dot(columns, piece, preferred_element_type=jnp.float32)
            total_sum = part if total_sum is None else total_sum + part
        return total_sum.astype(jnp.bfloat16)

    def send_home(step, node_sum):
        return shift(node_sum, n_node, -step)

    chunks = {0: jnp.concatenate([hidden_in, out_grad], axis=1)}
    received = {}
    contribs = {}
    sums = {}
    homes = {}
    for slot in range(-1, n_node + 2):
        produced = {}
        if 0 < slot + 2 < n_node:
            produced["chunk", slot + 2] = fetch(slot + 2, chunks[slot + 1])
        if 0 <= slot + 1 < n_node:
            produced["received", slot + 1] = send(slot + 1, chunks[slot + 1])
        if 0 <= slot < n_node:
            produced["contrib", slot] = compute(slot, received[slot])
        if 0 <= slot - 1 < n_node:
            produced["sum", slot - 1] = gather_back(slot - 1, contribs[slot - 1])
        if 0 <= slot - 2 < n_node:
            produced["home", slot - 2] = send_home(slot - 2, sums[slot - 2])
        keys = list(produced)
        values = lax.optimization_barrier([produced[key] for key in keys])
        for (kind, step), value in zip(keys, values):
            {"chunk": chunks, "received": received, "contrib": contribs, "sum": sums,
             "home": homes}[kind][step] = value

    total = homes[0].astype(jnp.float32)
    for step in range(1, n_node):
        total = total + homes[step].astype(jnp.float32)
    return total.astype(jnp.bfloat16)


def solution(mesh):
    in_specs = (
        P(("node", "local"), None),
        P(("node", "local"), None),
        P(None, "local", None),
        P(None, "local", None),
        P(("node", "local"), None),
        P(("node", "local"), None, None),
        P(("node", "local"), None, None),
    )
    out_specs = P(("node", "local"), None)
    return jax.shard_map(
        on_device, mesh=mesh, in_specs=in_specs, out_specs=out_specs, check_vma=False
    )
```

```python
import jax
import jax.numpy as jnp
from jax import lax
from jax.experimental import pallas as pl
from jax.sharding import PartitionSpec as P

FF = 1024
TOK_DEV = 128
TOPK = 8


def slot_ranks(ids, columns):
    slots = ids.shape[-1]
    onehot = (ids[..., None] == jnp.arange(columns, dtype=jnp.int32)).astype(jnp.bfloat16)
    order = jnp.arange(slots, dtype=jnp.int32)
    earlier = (order[:, None] > order[None, :]).astype(jnp.bfloat16)
    before = jnp.einsum("st,nte->nse", earlier, onehot, preferred_element_type=jnp.float32)
    return jnp.sum(before * onehot.astype(jnp.float32), axis=-1).astype(jnp.int32)


def part_kernel(grad_ref, weight_ref, out_ref):
    out_ref[...] = lax.dot_general(
        grad_ref[...], weight_ref[...], (((1,), (1,)), ((), ())),
        preferred_element_type=jnp.float32,
    ).astype(out_ref.dtype)


def part_matmul(grad_pre, weight_in):
    rows, depth = grad_pre.shape
    width = weight_in.shape[0]
    tile = 512 if width % 512 == 0 else width
    return pl.pallas_call(
        part_kernel,
        grid=(width // tile,),
        in_specs=[
            pl.BlockSpec((rows, depth), lambda j: (0, 0)),
            pl.BlockSpec((tile, depth), lambda j: (j, 0)),
        ],
        out_specs=pl.BlockSpec((rows, tile), lambda j: (0, j)),
        out_shape=jax.ShapeDtypeStruct((rows, width), jnp.bfloat16),
    )(grad_pre, weight_in)


def expert_backward(rows_x, rows_dy, rows_gate, saved, weight_in, weight_out):
    up_pre = jnp.dot(rows_x, weight_in[:, FF:], preferred_element_type=jnp.float32)
    grad_hidden = lax.dot_general(
        rows_dy, weight_out, (((1,), (1,)), ((), ())), preferred_element_type=jnp.float32
    )
    grad_hidden = grad_hidden * rows_gate.astype(jnp.float32)[:, None]
    gate_pre = saved.astype(jnp.float32)
    sigmoid_gate = jax.nn.sigmoid(gate_pre)
    grad_gate = grad_hidden * up_pre * sigmoid_gate * (1.0 + gate_pre * (1.0 - sigmoid_gate))
    grad_up = grad_hidden * gate_pre * sigmoid_gate
    grad_pre = jnp.concatenate([grad_gate, grad_up], axis=1).astype(jnp.bfloat16)
    return part_matmul(grad_pre, weight_in)


def select_rows(onehot, rows):
    picked = lax.dot_general(
        onehot, rows, (((0,), (0,)), ((), ())), preferred_element_type=jnp.float32
    )
    return picked.astype(jnp.bfloat16)


def shift(value, n_node, step):
    if step % n_node == 0:
        return value
    return lax.ppermute(value, "node", [(i, (i + step) % n_node) for i in range(n_node)])


def on_device(hidden_in, out_grad, expert_ids, gate_int, gate_saved, w_in, w_out):
    n_node = lax.axis_size("node")
    n_local = lax.axis_size("local")
    experts = n_node * n_local
    tok = hidden_in.shape[0]
    capacity = tok * TOPK // experts
    chunk_rows = n_local * capacity
    model_width = hidden_in.shape[1]
    node_here = lax.axis_index("node")
    weight_in = w_in[0]
    weight_out = w_out[0]

    ids = expert_ids.reshape(n_node, tok * TOPK)
    ranks = slot_ranks(ids, experts)
    on_here = (ids // n_local) == node_here
    position = jnp.where(on_here, (ids % n_local) * capacity + ranks, chunk_rows)
    weight = (gate_int.reshape(n_node, tok, TOPK).astype(jnp.float32) / 1024.0).astype(
        jnp.bfloat16
    )
    row_range = jnp.arange(chunk_rows, dtype=jnp.int32)

    sources = [(node_here - step) % n_node for step in range(n_node)]
    dispatch = []
    send_gate = []
    for step in range(n_node):
        chunk_pos = lax.dynamic_index_in_dim(position, sources[step], 0, keepdims=False)
        hits = (
            chunk_pos.reshape(tok, TOPK)[:, :, None] == row_range[None, None, :]
        ).astype(jnp.bfloat16)
        dispatch.append(jnp.sum(hits, axis=1))
        chunk_weight = lax.dynamic_index_in_dim(weight, sources[step], 0, keepdims=False)
        send_gate.append(
            jnp.einsum("tk,tkr->r", chunk_weight, hits, preferred_element_type=jnp.float32)
            .astype(jnp.bfloat16)
            .reshape(n_local, capacity)
        )
    gates = lax.all_to_all(jnp.stack(send_gate, axis=1), "local", 0, 0, tiled=True)

    def spread(rows):
        return lax.all_to_all(
            rows.reshape(n_local, capacity, rows.shape[-1]), "local", 0, 0, tiled=True
        )

    def fetch(step, previous):
        return shift(previous, n_node, 1)

    def send(step, chunk):
        return spread(select_rows(dispatch[step], chunk))

    def compute(step, received):
        saved = lax.dynamic_slice_in_dim(gate_saved, sources[step] * chunk_rows, chunk_rows, 0)
        rows = received.reshape(chunk_rows, 2 * model_width)
        return expert_backward(
            rows[:, :model_width],
            rows[:, model_width:],
            gates[:, step].reshape(chunk_rows),
            saved,
            weight_in,
            weight_out,
        )

    def gather_back(step, contrib):
        returned = spread(contrib).reshape(chunk_rows, model_width)
        return jnp.dot(dispatch[step], returned, preferred_element_type=jnp.float32).astype(
            jnp.bfloat16
        )

    def send_home(step, node_sum):
        return shift(node_sum, n_node, -step)

    chunks = {0: jnp.concatenate([hidden_in, out_grad], axis=1)}
    received = {}
    contribs = {}
    sums = {}
    homes = {}
    for slot in range(-1, n_node + 2):
        produced = {}
        if 0 < slot + 2 < n_node:
            produced["chunk", slot + 2] = fetch(slot + 2, chunks[slot + 1])
        if 0 <= slot + 1 < n_node:
            produced["received", slot + 1] = send(slot + 1, chunks[slot + 1])
        if 0 <= slot < n_node:
            produced["contrib", slot] = compute(slot, received[slot])
        if 0 <= slot - 1 < n_node:
            produced["sum", slot - 1] = gather_back(slot - 1, contribs[slot - 1])
        if 0 <= slot - 2 < n_node:
            produced["home", slot - 2] = send_home(slot - 2, sums[slot - 2])
        keys = list(produced)
        values = lax.optimization_barrier([produced[key] for key in keys])
        for (kind, step), value in zip(keys, values):
            {"chunk": chunks, "received": received, "contrib": contribs, "sum": sums,
             "home": homes}[kind][step] = value

    total = homes[0].astype(jnp.float32)
    for step in range(1, n_node):
        total = total + homes[step].astype(jnp.float32)
    return total.astype(jnp.bfloat16)


def solution(mesh):
    in_specs = (
        P(("node", "local"), None),
        P(("node", "local"), None),
        P(None, "local", None),
        P(None, "local", None),
        P(("node", "local"), None),
        P(("node", "local"), None, None),
        P(("node", "local"), None, None),
    )
    out_specs = P(("node", "local"), None)
    return jax.shard_map(
        on_device, mesh=mesh, in_specs=in_specs, out_specs=out_specs, check_vma=False
    )
```

```python
import jax
import jax.numpy as jnp
from jax import lax
from jax.experimental import pallas as pl
from jax.sharding import PartitionSpec as P

FF = 1024
TOK_DEV = 128
TOPK = 8


def slot_ranks(ids, columns):
    slots = ids.shape[-1]
    onehot = (ids[..., None] == jnp.arange(columns, dtype=jnp.int32)).astype(jnp.bfloat16)
    order = jnp.arange(slots, dtype=jnp.int32)
    earlier = (order[:, None] > order[None, :]).astype(jnp.bfloat16)
    before = jnp.einsum("st,nte->nse", earlier, onehot, preferred_element_type=jnp.float32)
    return jnp.sum(before * onehot.astype(jnp.float32), axis=-1).astype(jnp.int32)


def part_kernel(grad_ref, weight_ref, out_ref):
    out_ref[...] = jnp.dot(
        grad_ref[...], weight_ref[...], preferred_element_type=jnp.float32
    ).astype(out_ref.dtype)


def part_matmul(grad_pre, weight_in_t):
    rows, depth = grad_pre.shape
    width = weight_in_t.shape[1]
    tile = 512 if width % 512 == 0 else width
    return pl.pallas_call(
        part_kernel,
        grid=(width // tile,),
        in_specs=[
            pl.BlockSpec((rows, depth), lambda j: (0, 0)),
            pl.BlockSpec((depth, tile), lambda j: (0, j)),
        ],
        out_specs=pl.BlockSpec((rows, tile), lambda j: (0, j)),
        out_shape=jax.ShapeDtypeStruct((rows, width), jnp.bfloat16),
    )(grad_pre, weight_in_t)


def expert_backward(rows_x, rows_dy, rows_gate, saved, weight_in, weight_in_t, weight_out):
    up_pre = jnp.dot(rows_x, weight_in[:, FF:], preferred_element_type=jnp.float32)
    grad_hidden = lax.dot_general(
        rows_dy, weight_out, (((1,), (1,)), ((), ())), preferred_element_type=jnp.float32
    )
    grad_hidden = grad_hidden * rows_gate.astype(jnp.float32)[:, None]
    gate_pre = saved.astype(jnp.float32)
    sigmoid_gate = jax.nn.sigmoid(gate_pre)
    grad_gate = grad_hidden * up_pre * sigmoid_gate * (1.0 + gate_pre * (1.0 - sigmoid_gate))
    grad_up = grad_hidden * gate_pre * sigmoid_gate
    grad_pre = jnp.concatenate([grad_gate, grad_up], axis=1).astype(jnp.bfloat16)
    return part_matmul(grad_pre, weight_in_t)


def select_rows(onehot, rows):
    picked = lax.dot_general(
        onehot, rows, (((0,), (0,)), ((), ())), preferred_element_type=jnp.float32
    )
    return picked.astype(jnp.bfloat16)


def shift(value, n_node, step):
    if step % n_node == 0:
        return value
    return lax.ppermute(value, "node", [(i, (i + step) % n_node) for i in range(n_node)])


def on_device(hidden_in, out_grad, expert_ids, gate_int, gate_saved, w_in, w_out):
    n_node = lax.axis_size("node")
    n_local = lax.axis_size("local")
    experts = n_node * n_local
    tok = hidden_in.shape[0]
    capacity = tok * TOPK // experts
    chunk_rows = n_local * capacity
    model_width = hidden_in.shape[1]
    node_here = lax.axis_index("node")
    weight_in = w_in[0]
    weight_in_t = jnp.transpose(weight_in)
    weight_out = w_out[0]

    ids = expert_ids.reshape(n_node, tok * TOPK)
    ranks = slot_ranks(ids, experts)
    on_here = (ids // n_local) == node_here
    position = jnp.where(on_here, (ids % n_local) * capacity + ranks, chunk_rows)
    weight = (gate_int.reshape(n_node, tok, TOPK).astype(jnp.float32) / 1024.0).astype(
        jnp.bfloat16
    )
    row_range = jnp.arange(chunk_rows, dtype=jnp.int32)

    sources = [(node_here - step) % n_node for step in range(n_node)]
    dispatch = []
    send_gate = []
    for step in range(n_node):
        chunk_pos = lax.dynamic_index_in_dim(position, sources[step], 0, keepdims=False)
        hits = (
            chunk_pos.reshape(tok, TOPK)[:, :, None] == row_range[None, None, :]
        ).astype(jnp.bfloat16)
        dispatch.append(jnp.sum(hits, axis=1))
        chunk_weight = lax.dynamic_index_in_dim(weight, sources[step], 0, keepdims=False)
        send_gate.append(
            jnp.einsum("tk,tkr->r", chunk_weight, hits, preferred_element_type=jnp.float32)
            .astype(jnp.bfloat16)
            .reshape(n_local, capacity)
        )
    gates = lax.all_to_all(jnp.stack(send_gate, axis=1), "local", 0, 0, tiled=True)

    def spread(rows):
        return lax.all_to_all(
            rows.reshape(n_local, capacity, rows.shape[-1]), "local", 0, 0, tiled=True
        )

    def fetch(step, previous):
        return shift(previous, n_node, 1)

    def send(step, chunk):
        return spread(select_rows(dispatch[step], chunk))

    def compute(step, received):
        saved = lax.dynamic_slice_in_dim(gate_saved, sources[step] * chunk_rows, chunk_rows, 0)
        rows = received.reshape(chunk_rows, 2 * model_width)
        return expert_backward(
            rows[:, :model_width],
            rows[:, model_width:],
            gates[:, step].reshape(chunk_rows),
            saved,
            weight_in,
            weight_in_t,
            weight_out,
        )

    def gather_back(step, contrib):
        returned = spread(contrib).reshape(chunk_rows, model_width)
        return jnp.dot(dispatch[step], returned, preferred_element_type=jnp.float32).astype(
            jnp.bfloat16
        )

    def send_home(step, node_sum):
        return shift(node_sum, n_node, -step)

    chunks = {0: jnp.concatenate([hidden_in, out_grad], axis=1)}
    received = {}
    contribs = {}
    sums = {}
    homes = {}
    for slot in range(-1, n_node + 2):
        produced = {}
        if 0 < slot + 2 < n_node:
            produced["chunk", slot + 2] = fetch(slot + 2, chunks[slot + 1])
        if 0 <= slot + 1 < n_node:
            produced["received", slot + 1] = send(slot + 1, chunks[slot + 1])
        if 0 <= slot < n_node:
            produced["contrib", slot] = compute(slot, received[slot])
        if 0 <= slot - 1 < n_node:
            produced["sum", slot - 1] = gather_back(slot - 1, contribs[slot - 1])
        if 0 <= slot - 2 < n_node:
            produced["home", slot - 2] = send_home(slot - 2, sums[slot - 2])
        keys = list(produced)
        values = lax.optimization_barrier([produced[key] for key in keys])
        for (kind, step), value in zip(keys, values):
            {"chunk": chunks, "received": received, "contrib": contribs, "sum": sums,
             "home": homes}[kind][step] = value

    total = homes[0].astype(jnp.float32)
    for step in range(1, n_node):
        total = total + homes[step].astype(jnp.float32)
    return total.astype(jnp.bfloat16)


def solution(mesh):
    in_specs = (
        P(("node", "local"), None),
        P(("node", "local"), None),
        P(None, "local", None),
        P(None, "local", None),
        P(("node", "local"), None),
        P(("node", "local"), None, None),
        P(("node", "local"), None, None),
    )
    out_specs = P(("node", "local"), None)
    return jax.shard_map(
        on_device, mesh=mesh, in_specs=in_specs, out_specs=out_specs, check_vma=False
    )
```

```python
import jax
import jax.numpy as jnp
from jax import lax
from jax.experimental import pallas as pl
from jax.sharding import PartitionSpec as P

FF = 1024
TOK_DEV = 128
TOPK = 8


def slot_ranks(ids, columns):
    slots = ids.shape[-1]
    onehot = (ids[..., None] == jnp.arange(columns, dtype=jnp.int32)).astype(jnp.bfloat16)
    order = jnp.arange(slots, dtype=jnp.int32)
    earlier = (order[:, None] > order[None, :]).astype(jnp.bfloat16)
    before = jnp.einsum("st,nte->nse", earlier, onehot, preferred_element_type=jnp.float32)
    return jnp.sum(before * onehot.astype(jnp.float32), axis=-1).astype(jnp.int32)


def part_kernel(grad_ref, weight_ref, out_ref):
    out_ref[...] = lax.dot_general(
        grad_ref[...], weight_ref[...], (((1,), (1,)), ((), ())),
        preferred_element_type=jnp.float32,
    ).astype(out_ref.dtype)


def part_matmul(grad_pre, weight_in):
    rows, depth = grad_pre.shape
    width = weight_in.shape[0]
    tile = 512 if width % 512 == 0 else width
    return pl.pallas_call(
        part_kernel,
        grid=(width // tile,),
        in_specs=[
            pl.BlockSpec((rows, depth), lambda j: (0, 0)),
            pl.BlockSpec((tile, depth), lambda j: (j, 0)),
        ],
        out_specs=pl.BlockSpec((rows, tile), lambda j: (0, j)),
        out_shape=jax.ShapeDtypeStruct((rows, width), jnp.bfloat16),
    )(grad_pre, weight_in)


def expert_backward(rows_x, rows_dy, rows_gate, saved, weight_in, weight_out):
    up_pre = jnp.dot(rows_x, weight_in[:, FF:], preferred_element_type=jnp.float32)
    grad_hidden = lax.dot_general(
        rows_dy, weight_out, (((1,), (1,)), ((), ())), preferred_element_type=jnp.float32
    )
    grad_hidden = grad_hidden * rows_gate.astype(jnp.float32)[:, None]
    gate_pre = saved.astype(jnp.float32)
    sigmoid_gate = jax.nn.sigmoid(gate_pre)
    grad_gate = grad_hidden * up_pre * sigmoid_gate * (1.0 + gate_pre * (1.0 - sigmoid_gate))
    grad_up = grad_hidden * gate_pre * sigmoid_gate
    grad_pre = jnp.concatenate([grad_gate, grad_up], axis=1).astype(jnp.bfloat16)
    return part_matmul(grad_pre, weight_in)


def select_rows(onehot, rows):
    picked = lax.dot_general(
        onehot, rows, (((0,), (0,)), ((), ())), preferred_element_type=jnp.float32
    )
    return picked.astype(jnp.bfloat16)


def shift(value, n_node, step):
    if step % n_node == 0:
        return value
    return lax.ppermute(value, "node", [(i, (i + step) % n_node) for i in range(n_node)])


def on_device(hidden_in, out_grad, expert_ids, gate_int, gate_saved, w_in, w_out):
    n_node = lax.axis_size("node")
    n_local = lax.axis_size("local")
    experts = n_node * n_local
    tok = hidden_in.shape[0]
    capacity = tok * TOPK // experts
    chunk_rows = n_local * capacity
    model_width = hidden_in.shape[1]
    node_here = lax.axis_index("node")
    weight_in = w_in[0]
    weight_out = w_out[0]

    ids = expert_ids.reshape(n_node, tok * TOPK)
    ranks = slot_ranks(ids, experts)
    on_here = (ids // n_local) == node_here
    position = jnp.where(on_here, (ids % n_local) * capacity + ranks, chunk_rows)
    weight = (gate_int.reshape(n_node, tok, TOPK).astype(jnp.float32) / 1024.0).astype(
        jnp.bfloat16
    )
    row_range = jnp.arange(chunk_rows, dtype=jnp.int32)

    sources = [(node_here - step) % n_node for step in range(n_node)]
    dispatch = []
    send_gate = []
    for step in range(n_node):
        chunk_pos = lax.dynamic_index_in_dim(position, sources[step], 0, keepdims=False)
        hits = (
            chunk_pos.reshape(tok, TOPK)[:, :, None] == row_range[None, None, :]
        ).astype(jnp.bfloat16)
        dispatch.append(jnp.sum(hits, axis=1))
        chunk_weight = lax.dynamic_index_in_dim(weight, sources[step], 0, keepdims=False)
        send_gate.append(
            jnp.einsum("tk,tkr->r", chunk_weight, hits, preferred_element_type=jnp.float32)
            .astype(jnp.bfloat16)
            .reshape(n_local, capacity)
        )
    gates = lax.all_to_all(jnp.stack(send_gate, axis=1), "local", 0, 0, tiled=True)

    def spread(rows):
        return lax.all_to_all(
            rows.reshape(n_local, capacity, rows.shape[-1]), "local", 0, 0, tiled=True
        )

    def fetch(step, previous):
        return shift(previous, n_node, 1)

    def send(step, chunk):
        return spread(select_rows(dispatch[step], chunk))

    def compute(step, received):
        saved = lax.dynamic_slice_in_dim(gate_saved, sources[step] * chunk_rows, chunk_rows, 0)
        rows = received.reshape(chunk_rows, 2 * model_width)
        return expert_backward(
            rows[:, :model_width],
            rows[:, model_width:],
            gates[:, step].reshape(chunk_rows),
            saved,
            weight_in,
            weight_out,
        )

    def gather_back(step, contrib):
        returned = spread(contrib).reshape(chunk_rows, model_width)
        return jnp.dot(dispatch[step], returned, preferred_element_type=jnp.float32).astype(
            jnp.bfloat16
        )

    def send_home(step, node_sum):
        return shift(node_sum, n_node, -step)

    chunks = {0: jnp.concatenate([hidden_in, out_grad], axis=1)}
    received = {}
    contribs = {}
    homes = {}
    for slot in range(-1, n_node + 1):
        produced = {}
        if 0 < slot + 2 < n_node:
            produced["chunk", slot + 2] = fetch(slot + 2, chunks[slot + 1])
        if 0 <= slot + 1 < n_node:
            produced["received", slot + 1] = send(slot + 1, chunks[slot + 1])
        if 0 <= slot < n_node:
            produced["contrib", slot] = compute(slot, received[slot])
        if 0 <= slot - 1 < n_node:
            produced["home", slot - 1] = send_home(
                slot - 1, gather_back(slot - 1, contribs[slot - 1])
            )
        keys = list(produced)
        values = lax.optimization_barrier([produced[key] for key in keys])
        for (kind, step), value in zip(keys, values):
            {"chunk": chunks, "received": received, "contrib": contribs, "home": homes}[kind][
                step
            ] = value

    total = homes[0].astype(jnp.float32)
    for step in range(1, n_node):
        total = total + homes[step].astype(jnp.float32)
    return total.astype(jnp.bfloat16)


def solution(mesh):
    in_specs = (
        P(("node", "local"), None),
        P(("node", "local"), None),
        P(None, "local", None),
        P(None, "local", None),
        P(("node", "local"), None),
        P(("node", "local"), None, None),
        P(("node", "local"), None, None),
    )
    out_specs = P(("node", "local"), None)
    return jax.shard_map(
        on_device, mesh=mesh, in_specs=in_specs, out_specs=out_specs, check_vma=False
    )
```

```python
import jax
import jax.numpy as jnp
from jax import lax
from jax.experimental import pallas as pl
from jax.sharding import PartitionSpec as P

FF = 1024
TOK_DEV = 128
TOPK = 8


def slot_ranks(ids, columns):
    slots = ids.shape[-1]
    onehot = (ids[..., None] == jnp.arange(columns, dtype=jnp.int32)).astype(jnp.bfloat16)
    order = jnp.arange(slots, dtype=jnp.int32)
    earlier = (order[:, None] > order[None, :]).astype(jnp.bfloat16)
    before = jnp.einsum("st,nte->nse", earlier, onehot, preferred_element_type=jnp.float32)
    return jnp.sum(before * onehot.astype(jnp.float32), axis=-1).astype(jnp.int32)


def part_kernel(grad_ref, weight_ref, out_ref):
    out_ref[...] = lax.dot_general(
        grad_ref[...], weight_ref[...], (((1,), (1,)), ((), ())),
        preferred_element_type=jnp.float32,
    ).astype(out_ref.dtype)


def part_matmul(grad_pre, weight_in):
    rows, depth = grad_pre.shape
    width = weight_in.shape[0]
    tile = 512 if width % 512 == 0 else width
    return pl.pallas_call(
        part_kernel,
        grid=(width // tile,),
        in_specs=[
            pl.BlockSpec((rows, depth), lambda j: (0, 0)),
            pl.BlockSpec((tile, depth), lambda j: (j, 0)),
        ],
        out_specs=pl.BlockSpec((rows, tile), lambda j: (0, j)),
        out_shape=jax.ShapeDtypeStruct((rows, width), jnp.bfloat16),
    )(grad_pre, weight_in)


def expert_backward(rows_x, rows_dy, rows_gate, saved, weight_in, weight_out):
    up_pre = jnp.dot(rows_x, weight_in[:, FF:], preferred_element_type=jnp.float32)
    grad_hidden = lax.dot_general(
        rows_dy, weight_out, (((1,), (1,)), ((), ())), preferred_element_type=jnp.float32
    )
    grad_hidden = grad_hidden * rows_gate.astype(jnp.float32)[:, None]
    gate_pre = saved.astype(jnp.float32)
    sigmoid_gate = jax.nn.sigmoid(gate_pre)
    grad_gate = grad_hidden * up_pre * sigmoid_gate * (1.0 + gate_pre * (1.0 - sigmoid_gate))
    grad_up = grad_hidden * gate_pre * sigmoid_gate
    grad_pre = jnp.concatenate([grad_gate, grad_up], axis=1).astype(jnp.bfloat16)
    return part_matmul(grad_pre, weight_in)


def select_rows(onehot, rows):
    picked = lax.dot_general(
        onehot, rows, (((0,), (0,)), ((), ())), preferred_element_type=jnp.float32
    )
    return picked.astype(jnp.bfloat16)


def shift(value, n_node, step):
    if step % n_node == 0:
        return value
    return lax.ppermute(value, "node", [(i, (i + step) % n_node) for i in range(n_node)])


def on_device(hidden_in, out_grad, expert_ids, gate_int, gate_saved, w_in, w_out):
    n_node = lax.axis_size("node")
    n_local = lax.axis_size("local")
    experts = n_node * n_local
    tok = hidden_in.shape[0]
    capacity = tok * TOPK // experts
    chunk_rows = n_local * capacity
    model_width = hidden_in.shape[1]
    node_here = lax.axis_index("node")
    weight_in = w_in[0]
    weight_out = w_out[0]

    ids = expert_ids.reshape(n_node, tok * TOPK)
    ranks = slot_ranks(ids, experts)
    on_here = (ids // n_local) == node_here
    position = jnp.where(on_here, (ids % n_local) * capacity + ranks, chunk_rows)
    weight = (gate_int.reshape(n_node, tok, TOPK).astype(jnp.float32) / 1024.0).astype(
        jnp.bfloat16
    )
    row_range = jnp.arange(chunk_rows, dtype=jnp.int32)

    sources = [(node_here - step) % n_node for step in range(n_node)]
    dispatch = []
    send_gate = []
    for step in range(n_node):
        chunk_pos = lax.dynamic_index_in_dim(position, sources[step], 0, keepdims=False)
        hits = (
            chunk_pos.reshape(tok, TOPK)[:, :, None] == row_range[None, None, :]
        ).astype(jnp.bfloat16)
        dispatch.append(jnp.sum(hits, axis=1))
        chunk_weight = lax.dynamic_index_in_dim(weight, sources[step], 0, keepdims=False)
        send_gate.append(
            jnp.einsum("tk,tkr->r", chunk_weight, hits, preferred_element_type=jnp.float32)
            .astype(jnp.bfloat16)
            .reshape(n_local, capacity)
        )
    gate_store = {}

    def spread(rows):
        return lax.all_to_all(
            rows.reshape(n_local, capacity, rows.shape[-1]), "local", 0, 0, tiled=True
        )

    def fetch(step, previous):
        return shift(previous, n_node, 1)

    def send(step, chunk):
        return spread(select_rows(dispatch[step], chunk))

    def compute(step, received):
        saved = lax.dynamic_slice_in_dim(gate_saved, sources[step] * chunk_rows, chunk_rows, 0)
        rows = received.reshape(chunk_rows, 2 * model_width)
        return expert_backward(
            rows[:, :model_width],
            rows[:, model_width:],
            gate_store[0][:, step].reshape(chunk_rows),
            saved,
            weight_in,
            weight_out,
        )

    def gather_back(step, contrib):
        returned = spread(contrib).reshape(chunk_rows, model_width)
        return jnp.dot(dispatch[step], returned, preferred_element_type=jnp.float32).astype(
            jnp.bfloat16
        )

    def send_home(step, node_sum):
        return shift(node_sum, n_node, -step)

    chunks = {0: jnp.concatenate([hidden_in, out_grad], axis=1)}
    received = {}
    contribs = {}
    sums = {}
    homes = {}
    for slot in range(-1, n_node + 2):
        produced = {}
        if slot == -1:
            produced["gates", 0] = lax.all_to_all(
                jnp.stack(send_gate, axis=1), "local", 0, 0, tiled=True
            )
        if 0 < slot + 2 < n_node:
            produced["chunk", slot + 2] = fetch(slot + 2, chunks[slot + 1])
        if 0 <= slot + 1 < n_node:
            produced["received", slot + 1] = send(slot + 1, chunks[slot + 1])
        if 0 <= slot < n_node:
            produced["contrib", slot] = compute(slot, received[slot])
        if 0 <= slot - 1 < n_node:
            produced["sum", slot - 1] = gather_back(slot - 1, contribs[slot - 1])
        if 0 <= slot - 2 < n_node:
            produced["home", slot - 2] = send_home(slot - 2, sums[slot - 2])
        keys = list(produced)
        values = lax.optimization_barrier([produced[key] for key in keys])
        for (kind, step), value in zip(keys, values):
            {"chunk": chunks, "received": received, "contrib": contribs, "sum": sums,
             "home": homes, "gates": gate_store}[kind][step] = value

    total = homes[0].astype(jnp.float32)
    for step in range(1, n_node):
        total = total + homes[step].astype(jnp.float32)
    return total.astype(jnp.bfloat16)


def solution(mesh):
    in_specs = (
        P(("node", "local"), None),
        P(("node", "local"), None),
        P(None, "local", None),
        P(None, "local", None),
        P(("node", "local"), None),
        P(("node", "local"), None, None),
        P(("node", "local"), None, None),
    )
    out_specs = P(("node", "local"), None)
    return jax.shard_map(
        on_device, mesh=mesh, in_specs=in_specs, out_specs=out_specs, check_vma=False
    )
```

```python
import jax
import jax.numpy as jnp
from jax import lax
from jax.experimental import pallas as pl
from jax.sharding import PartitionSpec as P

FF = 1024
TOK_DEV = 128
TOPK = 8


def slot_ranks(ids, columns):
    slots = ids.shape[-1]
    onehot = (ids[..., None] == jnp.arange(columns, dtype=jnp.int32)).astype(jnp.bfloat16)
    order = jnp.arange(slots, dtype=jnp.int32)
    earlier = (order[:, None] > order[None, :]).astype(jnp.bfloat16)
    before = jnp.einsum("st,nte->nse", earlier, onehot, preferred_element_type=jnp.float32)
    return jnp.sum(before * onehot.astype(jnp.float32), axis=-1).astype(jnp.int32)


def part_kernel(grad_ref, weight_ref, out_ref):
    out_ref[...] = lax.dot_general(
        grad_ref[...], weight_ref[...], (((1,), (1,)), ((), ())),
        preferred_element_type=jnp.float32,
    ).astype(out_ref.dtype)


def part_matmul(grad_pre, weight_in):
    rows, depth = grad_pre.shape
    width = weight_in.shape[0]
    tile = 896 if width % 896 == 0 else width
    return pl.pallas_call(
        part_kernel,
        grid=(width // tile,),
        in_specs=[
            pl.BlockSpec((rows, depth), lambda j: (0, 0)),
            pl.BlockSpec((tile, depth), lambda j: (j, 0)),
        ],
        out_specs=pl.BlockSpec((rows, tile), lambda j: (0, j)),
        out_shape=jax.ShapeDtypeStruct((rows, width), jnp.bfloat16),
    )(grad_pre, weight_in)


def expert_backward(rows_x, rows_dy, rows_gate, saved, weight_in, weight_out):
    up_pre = jnp.dot(rows_x, weight_in[:, FF:], preferred_element_type=jnp.float32)
    grad_hidden = lax.dot_general(
        rows_dy, weight_out, (((1,), (1,)), ((), ())), preferred_element_type=jnp.float32
    )
    grad_hidden = grad_hidden * rows_gate.astype(jnp.float32)[:, None]
    gate_pre = saved.astype(jnp.float32)
    sigmoid_gate = jax.nn.sigmoid(gate_pre)
    grad_gate = grad_hidden * up_pre * sigmoid_gate * (1.0 + gate_pre * (1.0 - sigmoid_gate))
    grad_up = grad_hidden * gate_pre * sigmoid_gate
    grad_pre = jnp.concatenate([grad_gate, grad_up], axis=1).astype(jnp.bfloat16)
    return part_matmul(grad_pre, weight_in)


def select_rows(onehot, rows):
    picked = lax.dot_general(
        onehot, rows, (((0,), (0,)), ((), ())), preferred_element_type=jnp.float32
    )
    return picked.astype(jnp.bfloat16)


def shift(value, n_node, step):
    if step % n_node == 0:
        return value
    return lax.ppermute(value, "node", [(i, (i + step) % n_node) for i in range(n_node)])


def on_device(hidden_in, out_grad, expert_ids, gate_int, gate_saved, w_in, w_out):
    n_node = lax.axis_size("node")
    n_local = lax.axis_size("local")
    experts = n_node * n_local
    tok = hidden_in.shape[0]
    capacity = tok * TOPK // experts
    chunk_rows = n_local * capacity
    model_width = hidden_in.shape[1]
    node_here = lax.axis_index("node")
    weight_in = w_in[0]
    weight_out = w_out[0]

    ids = expert_ids.reshape(n_node, tok * TOPK)
    ranks = slot_ranks(ids, experts)
    on_here = (ids // n_local) == node_here
    position = jnp.where(on_here, (ids % n_local) * capacity + ranks, chunk_rows)
    weight = (gate_int.reshape(n_node, tok, TOPK).astype(jnp.float32) / 1024.0).astype(
        jnp.bfloat16
    )
    row_range = jnp.arange(chunk_rows, dtype=jnp.int32)

    sources = [(node_here - step) % n_node for step in range(n_node)]
    dispatch = []
    send_gate = []
    for step in range(n_node):
        chunk_pos = lax.dynamic_index_in_dim(position, sources[step], 0, keepdims=False)
        hits = (
            chunk_pos.reshape(tok, TOPK)[:, :, None] == row_range[None, None, :]
        ).astype(jnp.bfloat16)
        dispatch.append(jnp.sum(hits, axis=1))
        chunk_weight = lax.dynamic_index_in_dim(weight, sources[step], 0, keepdims=False)
        send_gate.append(
            jnp.einsum("tk,tkr->r", chunk_weight, hits, preferred_element_type=jnp.float32)
            .astype(jnp.bfloat16)
            .reshape(n_local, capacity)
        )
    gates = lax.all_to_all(jnp.stack(send_gate, axis=1), "local", 0, 0, tiled=True)

    def spread(rows):
        return lax.all_to_all(
            rows.reshape(n_local, capacity, rows.shape[-1]), "local", 0, 0, tiled=True
        )

    def fetch(step, previous):
        return shift(previous, n_node, 1)

    def send(step, chunk):
        return spread(select_rows(dispatch[step], chunk))

    def compute(step, received):
        saved = lax.dynamic_slice_in_dim(gate_saved, sources[step] * chunk_rows, chunk_rows, 0)
        rows = received.reshape(chunk_rows, 2 * model_width)
        return expert_backward(
            rows[:, :model_width],
            rows[:, model_width:],
            gates[:, step].reshape(chunk_rows),
            saved,
            weight_in,
            weight_out,
        )

    def gather_back(step, contrib):
        returned = spread(contrib).reshape(chunk_rows, model_width)
        return jnp.dot(dispatch[step], returned, preferred_element_type=jnp.float32).astype(
            jnp.bfloat16
        )

    def send_home(step, node_sum):
        return shift(node_sum, n_node, -step)

    chunks = {0: jnp.concatenate([hidden_in, out_grad], axis=1)}
    received = {}
    contribs = {}
    sums = {}
    homes = {}
    for slot in range(-1, n_node + 2):
        produced = {}
        if 0 < slot + 2 < n_node:
            produced["chunk", slot + 2] = fetch(slot + 2, chunks[slot + 1])
        if 0 <= slot + 1 < n_node:
            produced["received", slot + 1] = send(slot + 1, chunks[slot + 1])
        if 0 <= slot < n_node:
            produced["contrib", slot] = compute(slot, received[slot])
        if 0 <= slot - 1 < n_node:
            produced["sum", slot - 1] = gather_back(slot - 1, contribs[slot - 1])
        if 0 <= slot - 2 < n_node:
            produced["home", slot - 2] = send_home(slot - 2, sums[slot - 2])
        keys = list(produced)
        values = lax.optimization_barrier([produced[key] for key in keys])
        for (kind, step), value in zip(keys, values):
            {"chunk": chunks, "received": received, "contrib": contribs, "sum": sums,
             "home": homes}[kind][step] = value

    total = homes[0].astype(jnp.float32)
    for step in range(1, n_node):
        total = total + homes[step].astype(jnp.float32)
    return total.astype(jnp.bfloat16)


def solution(mesh):
    in_specs = (
        P(("node", "local"), None),
        P(("node", "local"), None),
        P(None, "local", None),
        P(None, "local", None),
        P(("node", "local"), None),
        P(("node", "local"), None, None),
        P(("node", "local"), None, None),
    )
    out_specs = P(("node", "local"), None)
    return jax.shard_map(
        on_device, mesh=mesh, in_specs=in_specs, out_specs=out_specs, check_vma=False
    )
```

```python
import jax
import jax.numpy as jnp
from jax import lax
from jax.experimental import pallas as pl
from jax.sharding import PartitionSpec as P

FF = 1024
TOK_DEV = 128
TOPK = 8


def slot_ranks(ids, columns):
    slots = ids.shape[-1]
    onehot = (ids[..., None] == jnp.arange(columns, dtype=jnp.int32)).astype(jnp.bfloat16)
    order = jnp.arange(slots, dtype=jnp.int32)
    earlier = (order[:, None] > order[None, :]).astype(jnp.bfloat16)
    before = jnp.einsum("st,nte->nse", earlier, onehot, preferred_element_type=jnp.float32)
    return jnp.sum(before * onehot.astype(jnp.float32), axis=-1).astype(jnp.int32)


def grad_kernel(x_ref, dy_ref, gate_ref, saved_ref, up_ref, out_w_ref, gate_out_ref, up_out_ref):
    up_pre = jnp.dot(x_ref[...], up_ref[...], preferred_element_type=jnp.float32)
    grad_hidden = lax.dot_general(
        dy_ref[...], out_w_ref[...], (((1,), (1,)), ((), ())),
        preferred_element_type=jnp.float32,
    ) * gate_ref[...].astype(jnp.float32)
    gate_pre = saved_ref[...].astype(jnp.float32)
    sigmoid_gate = 1.0 / (1.0 + jnp.exp(-gate_pre))
    gate_out_ref[...] = (
        grad_hidden * up_pre * sigmoid_gate * (1.0 + gate_pre * (1.0 - sigmoid_gate))
    ).astype(gate_out_ref.dtype)
    up_out_ref[...] = (grad_hidden * gate_pre * sigmoid_gate).astype(up_out_ref.dtype)


def grad_pre_halves(rows_x, rows_dy, rows_gate, saved, weight_in, weight_out):
    rows, width = rows_x.shape
    hidden = weight_out.shape[0]
    tile = 256 if hidden % 256 == 0 else hidden
    steps = hidden // tile
    return pl.pallas_call(
        grad_kernel,
        grid=(steps,),
        in_specs=[
            pl.BlockSpec((rows, width), lambda j: (0, 0)),
            pl.BlockSpec((rows, width), lambda j: (0, 0)),
            pl.BlockSpec((rows, 1), lambda j: (0, 0)),
            pl.BlockSpec((rows, tile), lambda j: (0, j)),
            pl.BlockSpec((width, tile), lambda j: (0, steps + j)),
            pl.BlockSpec((tile, width), lambda j: (j, 0)),
        ],
        out_specs=[
            pl.BlockSpec((rows, tile), lambda j: (0, j)),
            pl.BlockSpec((rows, tile), lambda j: (0, j)),
        ],
        out_shape=[jax.ShapeDtypeStruct((rows, hidden), jnp.bfloat16)] * 2,
    )(rows_x, rows_dy, rows_gate.reshape(rows, 1), saved, weight_in, weight_out)


def part_kernel(gate_ref, up_ref, weight_ref, out_ref):
    hidden = gate_ref.shape[1]
    contract = (((1,), (1,)), ((), ()))
    total = lax.dot_general(
        gate_ref[...], weight_ref[:, :hidden], contract, preferred_element_type=jnp.float32
    ) + lax.dot_general(
        up_ref[...], weight_ref[:, hidden:], contract, preferred_element_type=jnp.float32
    )
    out_ref[...] = total.astype(out_ref.dtype)


def part_matmul(grad_gate, grad_up, weight_in):
    rows, hidden = grad_gate.shape
    width = weight_in.shape[0]
    tile = 896 if width % 896 == 0 else width
    return pl.pallas_call(
        part_kernel,
        grid=(width // tile,),
        in_specs=[
            pl.BlockSpec((rows, hidden), lambda j: (0, 0)),
            pl.BlockSpec((rows, hidden), lambda j: (0, 0)),
            pl.BlockSpec((tile, 2 * hidden), lambda j: (j, 0)),
        ],
        out_specs=pl.BlockSpec((rows, tile), lambda j: (0, j)),
        out_shape=jax.ShapeDtypeStruct((rows, width), jnp.bfloat16),
    )(grad_gate, grad_up, weight_in)


def expert_backward(rows_x, rows_dy, rows_gate, saved, weight_in, weight_out):
    grad_gate, grad_up = grad_pre_halves(rows_x, rows_dy, rows_gate, saved, weight_in, weight_out)
    return part_matmul(grad_gate, grad_up, weight_in)


def select_rows(onehot, rows):
    picked = lax.dot_general(
        onehot, rows, (((0,), (0,)), ((), ())), preferred_element_type=jnp.float32
    )
    return picked.astype(jnp.bfloat16)


def shift(value, n_node, step):
    if step % n_node == 0:
        return value
    return lax.ppermute(value, "node", [(i, (i + step) % n_node) for i in range(n_node)])


def on_device(hidden_in, out_grad, expert_ids, gate_int, gate_saved, w_in, w_out):
    n_node = lax.axis_size("node")
    n_local = lax.axis_size("local")
    experts = n_node * n_local
    tok = hidden_in.shape[0]
    capacity = tok * TOPK // experts
    chunk_rows = n_local * capacity
    model_width = hidden_in.shape[1]
    node_here = lax.axis_index("node")
    weight_in = w_in[0]
    weight_out = w_out[0]

    ids = expert_ids.reshape(n_node, tok * TOPK)
    ranks = slot_ranks(ids, experts)
    on_here = (ids // n_local) == node_here
    position = jnp.where(on_here, (ids % n_local) * capacity + ranks, chunk_rows)
    weight = (gate_int.reshape(n_node, tok, TOPK).astype(jnp.float32) / 1024.0).astype(
        jnp.bfloat16
    )
    row_range = jnp.arange(chunk_rows, dtype=jnp.int32)

    sources = [(node_here - step) % n_node for step in range(n_node)]
    dispatch = []
    send_gate = []
    for step in range(n_node):
        chunk_pos = lax.dynamic_index_in_dim(position, sources[step], 0, keepdims=False)
        hits = (
            chunk_pos.reshape(tok, TOPK)[:, :, None] == row_range[None, None, :]
        ).astype(jnp.bfloat16)
        dispatch.append(jnp.sum(hits, axis=1))
        chunk_weight = lax.dynamic_index_in_dim(weight, sources[step], 0, keepdims=False)
        send_gate.append(
            jnp.einsum("tk,tkr->r", chunk_weight, hits, preferred_element_type=jnp.float32)
            .astype(jnp.bfloat16)
            .reshape(n_local, capacity)
        )
    gates = lax.all_to_all(jnp.stack(send_gate, axis=1), "local", 0, 0, tiled=True)

    def spread(rows):
        return lax.all_to_all(
            rows.reshape(n_local, capacity, rows.shape[-1]), "local", 0, 0, tiled=True
        )

    def fetch(step, previous):
        return shift(previous, n_node, 1)

    def send(step, chunk):
        return spread(select_rows(dispatch[step], chunk))

    def compute(step, received):
        saved = lax.dynamic_slice_in_dim(gate_saved, sources[step] * chunk_rows, chunk_rows, 0)
        rows = received.reshape(chunk_rows, 2 * model_width)
        return expert_backward(
            rows[:, :model_width],
            rows[:, model_width:],
            gates[:, step].reshape(chunk_rows),
            saved,
            weight_in,
            weight_out,
        )

    def gather_back(step, contrib):
        returned = spread(contrib).reshape(chunk_rows, model_width)
        return jnp.dot(dispatch[step], returned, preferred_element_type=jnp.float32).astype(
            jnp.bfloat16
        )

    def send_home(step, node_sum):
        return shift(node_sum, n_node, -step)

    chunks = {0: jnp.concatenate([hidden_in, out_grad], axis=1)}
    received = {}
    contribs = {}
    sums = {}
    homes = {}
    for slot in range(-1, n_node + 2):
        produced = {}
        if 0 < slot + 2 < n_node:
            produced["chunk", slot + 2] = fetch(slot + 2, chunks[slot + 1])
        if 0 <= slot + 1 < n_node:
            produced["received", slot + 1] = send(slot + 1, chunks[slot + 1])
        if 0 <= slot < n_node:
            produced["contrib", slot] = compute(slot, received[slot])
        if 0 <= slot - 1 < n_node:
            produced["sum", slot - 1] = gather_back(slot - 1, contribs[slot - 1])
        if 0 <= slot - 2 < n_node:
            produced["home", slot - 2] = send_home(slot - 2, sums[slot - 2])
        keys = list(produced)
        values = lax.optimization_barrier([produced[key] for key in keys])
        for (kind, step), value in zip(keys, values):
            {"chunk": chunks, "received": received, "contrib": contribs, "sum": sums,
             "home": homes}[kind][step] = value

    total = homes[0].astype(jnp.float32)
    for step in range(1, n_node):
        total = total + homes[step].astype(jnp.float32)
    return total.astype(jnp.bfloat16)


def solution(mesh):
    in_specs = (
        P(("node", "local"), None),
        P(("node", "local"), None),
        P(None, "local", None),
        P(None, "local", None),
        P(("node", "local"), None),
        P(("node", "local"), None, None),
        P(("node", "local"), None, None),
    )
    out_specs = P(("node", "local"), None)
    return jax.shard_map(
        on_device, mesh=mesh, in_specs=in_specs, out_specs=out_specs, check_vma=False
    )
```

```python
import jax
import jax.numpy as jnp
from jax import lax
from jax.experimental import pallas as pl
from jax.sharding import PartitionSpec as P

FF = 1024
TOK_DEV = 128
TOPK = 8


def slot_ranks(ids, columns):
    slots = ids.shape[-1]
    onehot = (ids[..., None] == jnp.arange(columns, dtype=jnp.int32)).astype(jnp.bfloat16)
    order = jnp.arange(slots, dtype=jnp.int32)
    earlier = (order[:, None] > order[None, :]).astype(jnp.bfloat16)
    before = jnp.einsum("st,nte->nse", earlier, onehot, preferred_element_type=jnp.float32)
    return jnp.sum(before * onehot.astype(jnp.float32), axis=-1).astype(jnp.int32)


def part_kernel(grad_ref, weight_ref, out_ref):
    out_ref[...] = lax.dot_general(
        grad_ref[...], weight_ref[...], (((1,), (1,)), ((), ())),
        preferred_element_type=jnp.float32,
    ).astype(out_ref.dtype)


def part_matmul(grad_pre, weight_in):
    rows, depth = grad_pre.shape
    width = weight_in.shape[0]
    tile = 896 if width % 896 == 0 else width
    return pl.pallas_call(
        part_kernel,
        grid=(width // tile,),
        in_specs=[
            pl.BlockSpec((rows, depth), lambda j: (0, 0)),
            pl.BlockSpec((tile, depth), lambda j: (j, 0)),
        ],
        out_specs=pl.BlockSpec((rows, tile), lambda j: (0, j)),
        out_shape=jax.ShapeDtypeStruct((rows, width), jnp.bfloat16),
    )(grad_pre, weight_in)


def expert_backward(rows_x, rows_dy, rows_gate, saved, weight_in, weight_out):
    up_pre = jnp.dot(rows_x, weight_in[:, FF:], preferred_element_type=jnp.float32)
    grad_hidden = lax.dot_general(
        rows_dy, weight_out, (((1,), (1,)), ((), ())), preferred_element_type=jnp.float32
    )
    grad_hidden = grad_hidden * rows_gate.astype(jnp.float32)[:, None]
    gate_pre = saved.astype(jnp.float32)
    sigmoid_gate = jax.nn.sigmoid(gate_pre)
    grad_gate = grad_hidden * up_pre * sigmoid_gate * (1.0 + gate_pre * (1.0 - sigmoid_gate))
    grad_up = grad_hidden * gate_pre * sigmoid_gate
    grad_pre = jnp.concatenate([grad_gate, grad_up], axis=1).astype(jnp.bfloat16)
    return part_matmul(grad_pre, weight_in)


def select_rows(onehot, rows):
    picked = lax.dot_general(
        onehot, rows, (((0,), (0,)), ((), ())), preferred_element_type=jnp.float32
    )
    return picked.astype(jnp.bfloat16)


def shift(value, n_node, step):
    if step % n_node == 0:
        return value
    return lax.ppermute(value, "node", [(i, (i + step) % n_node) for i in range(n_node)])


def on_device(hidden_in, out_grad, expert_ids, gate_int, gate_saved, w_in, w_out):
    n_node = lax.axis_size("node")
    n_local = lax.axis_size("local")
    experts = n_node * n_local
    tok = hidden_in.shape[0]
    capacity = tok * TOPK // experts
    chunk_rows = n_local * capacity
    model_width = hidden_in.shape[1]
    node_here = lax.axis_index("node")
    weight_in = w_in[0]
    weight_out = w_out[0]

    ids = expert_ids.reshape(n_node, tok * TOPK)
    ranks = slot_ranks(ids, experts)
    on_here = (ids // n_local) == node_here
    position = jnp.where(on_here, (ids % n_local) * capacity + ranks, chunk_rows)
    weight = (gate_int.reshape(n_node, tok, TOPK).astype(jnp.float32) / 1024.0).astype(
        jnp.bfloat16
    )
    row_range = jnp.arange(chunk_rows, dtype=jnp.int32)

    sources = [(node_here - step) % n_node for step in range(n_node)]
    dispatch = []
    send_gate = []
    for step in range(n_node):
        chunk_pos = lax.dynamic_index_in_dim(position, sources[step], 0, keepdims=False)
        hits = (
            chunk_pos.reshape(tok, TOPK)[:, :, None] == row_range[None, None, :]
        ).astype(jnp.bfloat16)
        dispatch.append(jnp.sum(hits, axis=1))
        chunk_weight = lax.dynamic_index_in_dim(weight, sources[step], 0, keepdims=False)
        send_gate.append(
            jnp.einsum("tk,tkr->r", chunk_weight, hits, preferred_element_type=jnp.float32)
            .astype(jnp.bfloat16)
            .reshape(n_local, capacity)
        )
    gate_columns = jnp.stack(send_gate, axis=-1)
    gate_columns = jnp.pad(gate_columns, ((0, 0), (0, 0), (0, 128 - n_node % 128)))
    gate_store = {}

    def spread(rows):
        return lax.all_to_all(
            rows.reshape(n_local, capacity, rows.shape[-1]), "local", 0, 0, tiled=True
        )

    def fetch(step, previous):
        return shift(previous, n_node, 1)

    def send(step, chunk):
        rows = select_rows(dispatch[step], chunk)
        if step == 0:
            rows = jnp.concatenate(
                [rows, gate_columns.reshape(chunk_rows, gate_columns.shape[-1])], axis=1
            )
        return spread(rows)

    def compute(step, received):
        saved = lax.dynamic_slice_in_dim(gate_saved, sources[step] * chunk_rows, chunk_rows, 0)
        rows = received.reshape(chunk_rows, received.shape[-1])
        if step == 0:
            gate_store[0] = rows[:, 2 * model_width : 2 * model_width + n_node]
        return expert_backward(
            rows[:, :model_width],
            rows[:, model_width : 2 * model_width],
            gate_store[0][:, step],
            saved,
            weight_in,
            weight_out,
        )

    def gather_back(step, contrib):
        returned = spread(contrib).reshape(chunk_rows, model_width)
        return jnp.dot(dispatch[step], returned, preferred_element_type=jnp.float32).astype(
            jnp.bfloat16
        )

    def send_home(step, node_sum):
        return shift(node_sum, n_node, -step)

    chunks = {0: jnp.concatenate([hidden_in, out_grad], axis=1)}
    received = {}
    contribs = {}
    sums = {}
    homes = {}
    for slot in range(-1, n_node + 2):
        produced = {}
        if 0 < slot + 2 < n_node:
            produced["chunk", slot + 2] = fetch(slot + 2, chunks[slot + 1])
        if 0 <= slot + 1 < n_node:
            produced["received", slot + 1] = send(slot + 1, chunks[slot + 1])
        if 0 <= slot < n_node:
            produced["contrib", slot] = compute(slot, received[slot])
        if 0 <= slot - 1 < n_node:
            produced["sum", slot - 1] = gather_back(slot - 1, contribs[slot - 1])
        if 0 <= slot - 2 < n_node:
            produced["home", slot - 2] = send_home(slot - 2, sums[slot - 2])
        keys = list(produced)
        values = lax.optimization_barrier([produced[key] for key in keys])
        for (kind, step), value in zip(keys, values):
            {"chunk": chunks, "received": received, "contrib": contribs, "sum": sums,
             "home": homes}[kind][step] = value

    total = homes[0].astype(jnp.float32)
    for step in range(1, n_node):
        total = total + homes[step].astype(jnp.float32)
    return total.astype(jnp.bfloat16)


def solution(mesh):
    in_specs = (
        P(("node", "local"), None),
        P(("node", "local"), None),
        P(None, "local", None),
        P(None, "local", None),
        P(("node", "local"), None),
        P(("node", "local"), None, None),
        P(("node", "local"), None, None),
    )
    out_specs = P(("node", "local"), None)
    return jax.shard_map(
        on_device, mesh=mesh, in_specs=in_specs, out_specs=out_specs, check_vma=False
    )
```

```python
import jax
import jax.numpy as jnp
from jax import lax
from jax.experimental import pallas as pl
from jax.sharding import PartitionSpec as P

FF = 1024
TOK_DEV = 128
TOPK = 8


def slot_ranks(ids, columns):
    slots = ids.shape[-1]
    onehot = (ids[..., None] == jnp.arange(columns, dtype=jnp.int32)).astype(jnp.bfloat16)
    order = jnp.arange(slots, dtype=jnp.int32)
    earlier = (order[:, None] > order[None, :]).astype(jnp.bfloat16)
    before = jnp.einsum("st,nte->nse", earlier, onehot, preferred_element_type=jnp.float32)
    return jnp.sum(before * onehot.astype(jnp.float32), axis=-1).astype(jnp.int32)


def part_kernel(grad_ref, weight_ref, out_ref):
    out_ref[...] = lax.dot_general(
        grad_ref[...], weight_ref[...], (((1,), (1,)), ((), ())),
        preferred_element_type=jnp.float32,
    ).astype(out_ref.dtype)


def part_matmul(grad_pre, weight_in):
    rows, depth = grad_pre.shape
    width = weight_in.shape[0]
    tile = 896 if width % 896 == 0 else width
    return pl.pallas_call(
        part_kernel,
        grid=(width // tile,),
        in_specs=[
            pl.BlockSpec((rows, depth), lambda j: (0, 0)),
            pl.BlockSpec((tile, depth), lambda j: (j, 0)),
        ],
        out_specs=pl.BlockSpec((rows, tile), lambda j: (0, j)),
        out_shape=jax.ShapeDtypeStruct((rows, width), jnp.bfloat16),
    )(grad_pre, weight_in)


def expert_backward(rows_x, rows_dy, rows_gate, saved, weight_in, weight_out):
    up_pre = jnp.dot(rows_x, weight_in[:, FF:], preferred_element_type=jnp.float32)
    grad_hidden = lax.dot_general(
        rows_dy, weight_out, (((1,), (1,)), ((), ())), preferred_element_type=jnp.float32
    )
    grad_hidden = grad_hidden * rows_gate.astype(jnp.float32)[:, None]
    gate_pre = saved.astype(jnp.float32)
    sigmoid_gate = jax.nn.sigmoid(gate_pre)
    grad_gate = grad_hidden * up_pre * sigmoid_gate * (1.0 + gate_pre * (1.0 - sigmoid_gate))
    grad_up = grad_hidden * gate_pre * sigmoid_gate
    grad_pre = jnp.concatenate([grad_gate, grad_up], axis=1).astype(jnp.bfloat16)
    return part_matmul(grad_pre, weight_in)


def select_rows(onehot, rows):
    picked = lax.dot_general(
        onehot, rows, (((0,), (0,)), ((), ())), preferred_element_type=jnp.float32
    )
    return picked.astype(jnp.bfloat16)


def shift(value, n_node, step):
    if step % n_node == 0:
        return value
    return lax.ppermute(value, "node", [(i, (i + step) % n_node) for i in range(n_node)])


def on_device(hidden_in, out_grad, expert_ids, gate_int, gate_saved, w_in, w_out):
    n_node = lax.axis_size("node")
    n_local = lax.axis_size("local")
    experts = n_node * n_local
    tok = hidden_in.shape[0]
    capacity = tok * TOPK // experts
    chunk_rows = n_local * capacity
    model_width = hidden_in.shape[1]
    node_here = lax.axis_index("node")
    weight_in = w_in[0]
    weight_out = w_out[0]

    ids = expert_ids.reshape(n_node, tok * TOPK)
    ranks = slot_ranks(ids, experts)
    on_here = (ids // n_local) == node_here
    position = jnp.where(on_here, (ids % n_local) * capacity + ranks, chunk_rows)
    weight = (gate_int.reshape(n_node, tok, TOPK).astype(jnp.float32) / 1024.0).astype(
        jnp.bfloat16
    )
    row_range = jnp.arange(chunk_rows, dtype=jnp.int32)

    sources = [(node_here - step) % n_node for step in range(n_node)]
    dispatch = []
    send_gate = []
    for step in range(n_node):
        chunk_pos = lax.dynamic_index_in_dim(position, sources[step], 0, keepdims=False)
        hits = (
            chunk_pos.reshape(tok, TOPK)[:, :, None] == row_range[None, None, :]
        ).astype(jnp.bfloat16)
        dispatch.append(jnp.sum(hits, axis=1))
        chunk_weight = lax.dynamic_index_in_dim(weight, sources[step], 0, keepdims=False)
        send_gate.append(
            jnp.einsum("tk,tkr->r", chunk_weight, hits, preferred_element_type=jnp.float32)
            .astype(jnp.bfloat16)
            .reshape(n_local, capacity)
        )
    gates = lax.all_to_all(jnp.stack(send_gate, axis=1), "local", 0, 0, tiled=True)

    def spread(rows):
        return lax.all_to_all(
            rows.reshape(n_local, capacity, rows.shape[-1]), "local", 0, 0, tiled=True
        )

    def fetch(step, previous):
        return shift(previous, n_node, 1)

    def send(step, chunk):
        return spread(select_rows(dispatch[step], chunk))

    def compute(step, received):
        saved = lax.dynamic_slice_in_dim(gate_saved, sources[step] * chunk_rows, chunk_rows, 0)
        rows = received.reshape(chunk_rows, 2 * model_width)
        return expert_backward(
            rows[:, :model_width],
            rows[:, model_width:],
            gates[:, step].reshape(chunk_rows),
            saved,
            weight_in,
            weight_out,
        )

    def gather_back(step, contrib):
        returned = spread(contrib).reshape(chunk_rows, model_width)
        return jnp.dot(dispatch[step], returned, preferred_element_type=jnp.float32).astype(
            jnp.bfloat16
        )

    def send_home(step, node_sum):
        return shift(node_sum, n_node, -step)

    chunks = {0: jnp.concatenate([hidden_in, out_grad], axis=1)}
    for step in range(1, n_node):
        chunks[step] = fetch(step, chunks[step - 1])
    received = {}
    contribs = {}
    sums = {}
    homes = {}
    for slot in range(-1, n_node + 2):
        produced = {}
        if 0 <= slot + 1 < n_node:
            produced["received", slot + 1] = send(slot + 1, chunks[slot + 1])
        if 0 <= slot < n_node:
            produced["contrib", slot] = compute(slot, received[slot])
        if 0 <= slot - 1 < n_node:
            produced["sum", slot - 1] = gather_back(slot - 1, contribs[slot - 1])
        if 0 <= slot - 2 < n_node:
            produced["home", slot - 2] = send_home(slot - 2, sums[slot - 2])
        keys = list(produced)
        values = lax.optimization_barrier([produced[key] for key in keys])
        for (kind, step), value in zip(keys, values):
            {"chunk": chunks, "received": received, "contrib": contribs, "sum": sums,
             "home": homes}[kind][step] = value

    total = homes[0].astype(jnp.float32)
    for step in range(1, n_node):
        total = total + homes[step].astype(jnp.float32)
    return total.astype(jnp.bfloat16)


def solution(mesh):
    in_specs = (
        P(("node", "local"), None),
        P(("node", "local"), None),
        P(None, "local", None),
        P(None, "local", None),
        P(("node", "local"), None),
        P(("node", "local"), None, None),
        P(("node", "local"), None, None),
    )
    out_specs = P(("node", "local"), None)
    return jax.shard_map(
        on_device, mesh=mesh, in_specs=in_specs, out_specs=out_specs, check_vma=False
    )
```

```python
import jax
import jax.numpy as jnp
from jax import lax
from jax.experimental import pallas as pl
from jax.sharding import PartitionSpec as P

FF = 1024
TOK_DEV = 128
TOPK = 8


def slot_ranks(ids, columns):
    slots = ids.shape[-1]
    onehot = (ids[..., None] == jnp.arange(columns, dtype=jnp.int32)).astype(jnp.bfloat16)
    order = jnp.arange(slots, dtype=jnp.int32)
    earlier = (order[:, None] > order[None, :]).astype(jnp.bfloat16)
    before = jnp.einsum("st,nte->nse", earlier, onehot, preferred_element_type=jnp.float32)
    return jnp.sum(before * onehot.astype(jnp.float32), axis=-1).astype(jnp.int32)


def part_kernel(grad_ref, weight_ref, out_ref):
    out_ref[...] = lax.dot_general(
        grad_ref[...], weight_ref[...], (((1,), (1,)), ((), ())),
        preferred_element_type=jnp.float32,
    ).astype(out_ref.dtype)


def part_matmul(grad_pre, weight_in):
    rows, depth = grad_pre.shape
    width = weight_in.shape[0]
    tile = 896 if width % 896 == 0 else width
    return pl.pallas_call(
        part_kernel,
        grid=(width // tile,),
        in_specs=[
            pl.BlockSpec((rows, depth), lambda j: (0, 0)),
            pl.BlockSpec((tile, depth), lambda j: (j, 0)),
        ],
        out_specs=pl.BlockSpec((rows, tile), lambda j: (0, j)),
        out_shape=jax.ShapeDtypeStruct((rows, width), jnp.bfloat16),
    )(grad_pre, weight_in)


def expert_backward(rows_x, rows_dy, rows_gate, saved, weight_in, weight_out):
    up_pre = jnp.dot(rows_x, weight_in[:, FF:], preferred_element_type=jnp.float32)
    grad_hidden = lax.dot_general(
        rows_dy, weight_out, (((1,), (1,)), ((), ())), preferred_element_type=jnp.float32
    )
    grad_hidden = grad_hidden * rows_gate.astype(jnp.float32)[:, None]
    gate_pre = saved.astype(jnp.float32)
    sigmoid_gate = jax.nn.sigmoid(gate_pre)
    grad_gate = grad_hidden * up_pre * sigmoid_gate * (1.0 + gate_pre * (1.0 - sigmoid_gate))
    grad_up = grad_hidden * gate_pre * sigmoid_gate
    grad_pre = jnp.concatenate([grad_gate, grad_up], axis=1).astype(jnp.bfloat16)
    return part_matmul(grad_pre, weight_in)


def select_rows(onehot, rows):
    picked = lax.dot_general(
        onehot, rows, (((0,), (0,)), ((), ())), preferred_element_type=jnp.float32
    )
    return picked.astype(jnp.bfloat16)


def shift(value, n_node, step):
    if step % n_node == 0:
        return value
    return lax.ppermute(value, "node", [(i, (i + step) % n_node) for i in range(n_node)])


def on_device(hidden_in, out_grad, expert_ids, gate_int, gate_saved, w_in, w_out):
    n_node = lax.axis_size("node")
    n_local = lax.axis_size("local")
    experts = n_node * n_local
    tok = hidden_in.shape[0]
    capacity = tok * TOPK // experts
    chunk_rows = n_local * capacity
    model_width = hidden_in.shape[1]
    node_here = lax.axis_index("node")
    weight_in = w_in[0]
    weight_out = w_out[0]

    ids = expert_ids.reshape(n_node, tok * TOPK)
    ranks = slot_ranks(ids, experts)
    on_here = (ids // n_local) == node_here
    position = jnp.where(on_here, (ids % n_local) * capacity + ranks, chunk_rows)
    weight = (gate_int.reshape(n_node, tok, TOPK).astype(jnp.float32) / 1024.0).astype(
        jnp.bfloat16
    )
    row_range = jnp.arange(chunk_rows, dtype=jnp.int32)

    sources = [(node_here - step) % n_node for step in range(n_node)]
    dispatch = []
    send_gate = []
    for step in range(n_node):
        chunk_pos = lax.dynamic_index_in_dim(position, sources[step], 0, keepdims=False)
        hits = (
            chunk_pos.reshape(tok, TOPK)[:, :, None] == row_range[None, None, :]
        ).astype(jnp.bfloat16)
        dispatch.append(jnp.sum(hits, axis=1))
        chunk_weight = lax.dynamic_index_in_dim(weight, sources[step], 0, keepdims=False)
        send_gate.append(
            jnp.einsum("tk,tkr->r", chunk_weight, hits, preferred_element_type=jnp.float32)
            .astype(jnp.bfloat16)
            .reshape(n_local, capacity)
        )
    gates = lax.all_to_all(jnp.stack(send_gate, axis=1), "local", 0, 0, tiled=True)

    def spread(rows):
        return lax.all_to_all(
            rows.reshape(n_local, capacity, rows.shape[-1]), "local", 0, 0, tiled=True
        )

    def fetch(step, previous):
        return shift(previous, n_node, 1)

    def send(step, chunk):
        return spread(select_rows(dispatch[step], chunk))

    def compute(step, received):
        saved = lax.dynamic_slice_in_dim(gate_saved, sources[step] * chunk_rows, chunk_rows, 0)
        rows = received.reshape(chunk_rows, 2 * model_width)
        return expert_backward(
            rows[:, :model_width],
            rows[:, model_width:],
            gates[:, step].reshape(chunk_rows),
            saved,
            weight_in,
            weight_out,
        )

    def gather_back(step, contrib):
        returned = spread(contrib).reshape(chunk_rows, model_width)
        return jnp.dot(dispatch[step], returned, preferred_element_type=jnp.float32).astype(
            jnp.bfloat16
        )

    def send_home(step, node_sum):
        return shift(node_sum, n_node, -step)

    chunks = {0: jnp.concatenate([hidden_in, out_grad], axis=1)}
    received = {}
    contribs = {}
    sums = {}
    homes = {}
    for slot in range(-1, n_node + 2):
        produced = {}
        if 0 < slot + 2 < n_node:
            produced["chunk", slot + 2] = fetch(slot + 2, chunks[slot + 1])
        if 0 <= slot + 1 < n_node:
            produced["received", slot + 1] = send(slot + 1, chunks[slot + 1])
        if 0 <= slot < n_node:
            produced["contrib", slot] = compute(slot, received[slot])
        if 0 <= slot - 1 < n_node:
            node_sum = gather_back(slot - 1, contribs[slot - 1])
            if slot - 1 == n_node - 2:
                produced["home", slot - 1] = send_home(slot - 1, node_sum)
            else:
                produced["sum", slot - 1] = node_sum
        if 0 <= slot - 2 < n_node and slot - 2 != n_node - 2:
            produced["home", slot - 2] = send_home(slot - 2, sums[slot - 2])
        keys = list(produced)
        values = lax.optimization_barrier([produced[key] for key in keys])
        for (kind, step), value in zip(keys, values):
            {"chunk": chunks, "received": received, "contrib": contribs, "sum": sums,
             "home": homes}[kind][step] = value

    total = homes[0].astype(jnp.float32)
    for step in range(1, n_node):
        total = total + homes[step].astype(jnp.float32)
    return total.astype(jnp.bfloat16)


def solution(mesh):
    in_specs = (
        P(("node", "local"), None),
        P(("node", "local"), None),
        P(None, "local", None),
        P(None, "local", None),
        P(("node", "local"), None),
        P(("node", "local"), None, None),
        P(("node", "local"), None, None),
    )
    out_specs = P(("node", "local"), None)
    return jax.shard_map(
        on_device, mesh=mesh, in_specs=in_specs, out_specs=out_specs, check_vma=False
    )
```
